256 devices in a mesh: seq: 32 (over x, z), mp: 8 (over y, core).
Axes of the slice: x: 4, y: 4, z: 8, core: 2. Of those that a mesh axis runs over, the one named last changes fastest.
Arguments:
- tokens: bfloat16 [12288, 1792], P('seq'), may hold values from -6 to 6
- prompt_lengths: int32 [4], replicated, may hold values from 1 to 9216, 12288 in all
- norm_mixer: bfloat16 [1792], replicated, may hold values from 0.25 to 1.75
- norm_conv: bfloat16 [1792], replicated, may hold values from 0.25 to 1.75
- norm_mlp: bfloat16 [1792], replicated, may hold values from 0.25 to 1.75
- w_query: bfloat16 [1792, 256], P(None, 'mp'), may hold values from -0.125 to 0.125
- w_key: bfloat16 [1792, 256], P(None, 'mp'), may hold values from -0.125 to 0.125
- w_value: bfloat16 [1792, 1792], P(None, 'mp'), may hold values from -0.125 to 0.125
- w_out: bfloat16 [1792, 1792], P('mp'), may hold values from -0.125 to 0.125
- w_proj: bfloat16 [1792, 1792], P(None, 'mp'), may hold values from -0.125 to 0.125
- conv_kernel: bfloat16 [3, 1792], P(None, 'mp'), may hold values from -3 to 3
- w_gate: bfloat16 [1792, 4864], P(None, 'mp'), may hold values from -0.125 to 0.125
- w_up: bfloat16 [1792, 4864], P(None, 'mp'), may hold values from -0.125 to 0.125
- w_down: bfloat16 [4864, 1792], P('mp'), may hold values from -0.078125 to 0.078125
Outputs:
- hidden_out: bfloat16 [12288, 1792], P('seq')
- cache_state: float32 [32, 16, 273, 112], P('seq', 'mp')
- cache_norm: float32 [32, 16, 273], P('seq', 'mp')
The draws below stay inside these ranges and needn't reach their ends.
Inputs may be any that keep to these rules, and one draw needn't show every extreme that they name: `prompt_lengths`: the 4 prompts fill the pack in order and sum to 12288; the longest has exactly 9216 tokens.
All inputs are finite; a program needn't handle non-finite values.
Results may differ from the reference program's by a relative error of at most 0.02.
Values may be sent and summed in bfloat16 or wider, within the bound.
No kernel may reach another device: no remote copies, remote signals or barrier semaphores. Data moves between devices by JAX's collectives and lax.ppermute only.
A program may use at most 128 MiB of HBM per device.

```python
import math
import jax
import jax.numpy as jnp
import numpy as np
from jax import lax

D = 1792
H = 16
F = 16
DV = 112
FF = 4864
KC = 3
NDOC = 4
TOK_DEV = 384
FEAT = 273
TOKENS = 12288
MOSTLEN = 9216
N_SEQ = 32
N_MP = 8


def draw_tokens(key, part):
    noise_key = jax.random.fold_in(key, 11)
    offset_key = jax.random.fold_in(key, 23)
    noise = 0.6 * jax.random.normal(noise_key, (TOKENS, D), jnp.float32)
    offset = 0.8 * jax.random.normal(offset_key, (TOKENS // TOK_DEV, D), jnp.float32)
    rows = jnp.repeat(offset, TOK_DEV, axis=0)
    return jnp.clip(noise + rows, -6.0, 6.0).astype(jnp.bfloat16)


def block_scale(key, extent, shards, low, top_value):
    level = 1.0
    for position, parts in shards:
        heights = jax.random.uniform(jax.random.fold_in(jax.random.fold_in(key, 6), position), (parts,), jnp.float32, low / len(shards), top_value / len(shards))
        level = level * jnp.repeat(jnp.exp(heights), extent[position] // parts).reshape((-1,) + (1,) * (len(extent) - 1 - position))
    return level


def split_up(count, total, reach, lean):
    loads = [(1 << 20) // math.isqrt(standing ** lean) + 1 for standing in range(2, count + 1)]
    surplus, given = total - reach - (count - 1), [1] * (count - 1)
    while surplus > 0:
        candidates = [i for i in range(count - 1) if given[i] < reach]
        whole, remaining = sum([loads[i] for i in candidates]), surplus
        for i in candidates:
            extra = min(reach - given[i], max(1, remaining * loads[i] // whole), surplus)
            given[i] = given[i] + extra
            surplus = surplus - extra
    return np.array([reach] + given)


def ragged_sizes(key, amount, total, most, slope):
    if amount == 2:
        one = jax.random.randint(key, (), max(1, total - most), min(most, total - 1) + 1)
        return jnp.stack([one, total - one])
    lengths = jnp.asarray(split_up(amount, total, most, slope), jnp.int32)
    twos = (amount - 1) // 2
    source_of, taker = lengths[1:1 + 2 * twos:2], lengths[2:2 + 2 * twos:2]
    room = jnp.minimum(source_of - 1, most - taker)
    moved = jax.random.randint(jax.random.fold_in(key, 1), (twos,), 0, 1 << 20) % (room + 1)
    lengths = lengths.at[1:1 + 2 * twos:2].set(source_of - moved).at[2:2 + 2 * twos:2].set(taker + moved)
    return lengths[jax.random.permutation(jax.random.fold_in(key, 2), amount)]


def centred(stream_key, dims, scale, limit, split=(), kind=jnp.bfloat16):
    level = block_scale(stream_key, dims, split, -0.22, 0.18) if split else 1.0
    values = jax.random.normal(stream_key, dims, jnp.float32) * scale * level
    return jnp.minimum(jnp.maximum(values, -limit), limit).astype(kind)


def setup_inputs(seed: int = 0) -> dict:
    splits = jax.random.split(jax.random.key(seed), 15)
    tokens = draw_tokens(jax.random.fold_in(splits[14], 71), 0)
    prompt_lengths = ragged_sizes(splits[1], NDOC, TOKENS, MOSTLEN, 2).astype(jnp.int32)
    norm_mixer = jnp.clip(1.0 + 0.15 * jax.random.normal(splits[2], (D,), jnp.float32), 0.25, 1.75).astype(jnp.bfloat16)
    norm_conv = jnp.clip(1.0 + 0.15 * jax.random.normal(splits[3], (D,), jnp.float32), 0.25, 1.75).astype(jnp.bfloat16)
    norm_mlp = jnp.clip(1.0 + 0.15 * jax.random.normal(splits[4], (D,), jnp.float32), 0.25, 1.75).astype(jnp.bfloat16)
    w_query = centred(splits[5], (D, H * F), D ** -0.5, 0.125, ((1, 8),))
    w_key = centred(splits[6], (D, H * F), D ** -0.5, 0.125, ((1, 8),))
    w_value = centred(splits[7], (D, H * DV), D ** -0.5, 0.125, ((1, 8),))
    w_out = centred(splits[8], (H * DV, D), D ** -0.5, 0.125, ((0, 8),))
    w_proj = centred(splits[9], (D, D), D ** -0.5, 0.125, ((1, 8),))
    conv_kernel = centred(splits[10], (KC, D), 0.6, 3.0, ((1, 8),))
    w_gate = centred(splits[11], (D, FF), D ** -0.5, 0.125, ((1, 8),))
    w_up = centred(splits[12], (D, FF), D ** -0.5, 0.125, ((1, 8),))
    w_down = centred(splits[13], (FF, D), FF ** -0.5, 0.078125, ((0, 8),))
    return dict(tokens=tokens, prompt_lengths=prompt_lengths, norm_mixer=norm_mixer, norm_conv=norm_conv, norm_mlp=norm_mlp, w_query=w_query, w_key=w_key, w_value=w_value, w_out=w_out, w_proj=w_proj, conv_kernel=conv_kernel, w_gate=w_gate, w_up=w_up, w_down=w_down)


def norm_rows(values, gain):
    mean_sq = lax.optimization_barrier(jnp.mean(values * values, axis=-1, keepdims=True))
    return values * lax.rsqrt(mean_sq + 1e-06) * gain.astype(jnp.float32)

def features(heads_in):
    scaled = heads_in.astype(jnp.float32) * F ** (-0.25)
    outer = scaled[..., :, None] * scaled[..., None, :]
    outer = outer.reshape(scaled.shape[:-1] + (F * F,)) / jnp.sqrt(jnp.float32(2.0))
    ones = jnp.ones(scaled.shape[:-1] + (1,), jnp.float32)
    return jnp.concatenate([ones, scaled, outer], axis=-1)

def round_trip(values):
    return lax.optimization_barrier(values.astype(jnp.bfloat16)).astype(jnp.float32)

def reference(tokens, prompt_lengths, norm_mixer, norm_conv, norm_mlp, w_query, w_key, w_value, w_out, w_proj, conv_kernel, w_gate, w_up, w_down):
    hidden_projection = lax.Precision.HIGHEST
    ends = jnp.cumsum(prompt_lengths).astype(jnp.int32)
    place = jnp.arange(TOKENS, dtype=jnp.int32)
    below = ends[None, :] <= place[:, None]
    doc = lax.optimization_barrier(jnp.sum(below.astype(jnp.int32), axis=1)).astype(jnp.int32)
    start = lax.optimization_barrier(jnp.max(jnp.where(below, ends[None, :], 0), axis=1)).astype(jnp.int32)
    resid = tokens.astype(jnp.float32)
    n1 = norm_rows(resid, norm_mixer).astype(jnp.bfloat16)
    query = jnp.dot(n1, w_query, preferred_element_type=jnp.float32).astype(jnp.bfloat16).reshape(TOKENS, H, F)
    keys = jnp.dot(n1, w_key, preferred_element_type=jnp.float32).astype(jnp.bfloat16).reshape(TOKENS, H, F)
    values = jnp.dot(n1, w_value, preferred_element_type=jnp.float32).astype(jnp.bfloat16).reshape(TOKENS, H, DV)
    blocks = (query.reshape(N_SEQ, TOK_DEV, H, F), keys.reshape(N_SEQ, TOK_DEV, H, F), values.reshape(N_SEQ, TOK_DEV, H, DV), doc.reshape(N_SEQ, TOK_DEV), start.reshape(N_SEQ, TOK_DEV), place.reshape(N_SEQ, TOK_DEV))

    def one_block(carry, item):
        state, znorm, last = carry
        qb, kb, vb, db, sb, pb = item
        qf = qb.astype(jnp.float32)
        kf = kb.astype(jnp.float32)
        value_float_rows = vb.astype(jnp.float32)
        score = jnp.einsum('nhf,mhf->hnm', qf, kf, precision=hidden_projection) * F ** (-0.5)
        weight_matrix = 1.0 + score + 0.5 * score * score
        mask = (pb[None, :] <= pb[:, None]) & (pb[None, :] >= sb[:, None])
        weight_matrix = weight_matrix * mask.astype(jnp.float32)[None]
        numerator_term = jnp.einsum('obg,goq->boq', weight_matrix, value_float_rows, precision=hidden_projection)
        denom = lax.optimization_barrier(jnp.sum(weight_matrix, axis=2)).T
        phiq = features(qb)
        apply = (db == last).astype(jnp.float32)
        numerator_term = numerator_term + jnp.einsum('nhe,hed->nhd', phiq, state, precision=hidden_projection) * apply[:, None, None]
        denom = denom + jnp.einsum('nhe,he->nh', phiq, znorm, precision=hidden_projection) * apply[:, None]
        attn_block = (numerator_term / denom[:, :, None]).astype(jnp.bfloat16)
        tail = (db == db[-1]).astype(jnp.float32)
        key_feature_map = features(kb) * tail[:, None, None]
        trailing_state = jnp.einsum('fcs,fcz->csz', key_feature_map, value_float_rows, precision=hidden_projection)
        tail_norm = lax.optimization_barrier(jnp.sum(key_feature_map, axis=0))
        cont = (db[0] == db[-1]) & (last == db[0])
        new_state = trailing_state + jnp.where(cont, state, jnp.zeros_like(state))
        new_norm = tail_norm + jnp.where(cont, znorm, jnp.zeros_like(znorm))
        count = (pb[-1] + 1 - sb[-1]).astype(jnp.float32)
        return ((new_state, new_norm, db[-1]), (attn_block, new_state / count, new_norm / count))
    init = (jnp.zeros((H, FEAT, DV), jnp.float32), jnp.zeros((H, FEAT), jnp.float32), jnp.array(-1, jnp.int32))
    _, (attn, cache_state, cache_norm) = lax.scan(one_block, init, blocks)
    attn = attn.reshape(TOKENS, H * DV)
    group = H * DV // N_MP
    mixed = jnp.zeros((TOKENS, D), jnp.float32)
    for g in range(N_MP):
        term = jnp.dot(attn[:, g * group:(g + 1) * group], w_out[g * group:(g + 1) * group], preferred_element_type=jnp.float32)
        mixed = mixed + round_trip(term)
    res1 = resid + mixed
    n2 = norm_rows(res1, norm_conv).astype(jnp.bfloat16)
    proj = jnp.dot(n2, w_proj, preferred_element_type=jnp.float32)
    padded = jnp.concatenate([jnp.zeros((KC - 1, D), jnp.float32), n2.astype(jnp.float32)], axis=0)
    conv = jnp.zeros((TOKENS, D), jnp.float32)
    for tap in range(KC):
        keep = (place - tap >= start).astype(jnp.float32)
        conv = conv + conv_kernel[tap].astype(jnp.float32)[None, :] * padded[KC - 1 - tap:KC - 1 - tap + TOKENS] * keep[:, None]
    gated = (proj * conv).astype(jnp.bfloat16)
    res2 = res1 + gated.astype(jnp.float32)
    n3 = norm_rows(res2, norm_mlp).astype(jnp.bfloat16)
    gate = jnp.dot(n3, w_gate, preferred_element_type=jnp.float32)
    upper = jnp.dot(n3, w_up, preferred_element_type=jnp.float32)
    hid = (jax.nn.silu(gate) * upper).astype(jnp.bfloat16)
    width = FF // N_MP
    down = jnp.zeros((TOKENS, D), jnp.float32)
    for g in range(N_MP):
        term = jnp.dot(hid[:, g * width:(g + 1) * width], w_down[g * width:(g + 1) * width], preferred_element_type=jnp.float32)
        down = down + round_trip(term)
    hidden_out = (res2 + down).astype(jnp.bfloat16)
    return (hidden_out, cache_state, cache_norm)
```

```python
import jax
import jax.numpy as jnp
import numpy as np
from jax import lax
from jax.sharding import PartitionSpec as P

F = 16
DV = 112
KC = 3
FEAT = 273

PAIR_A, PAIR_B = np.triu_indices(F)
NPAIR = PAIR_A.shape[0]
NCOMP = 1 + F + NPAIR
PAIR_W = np.where(PAIR_A == PAIR_B, 0.5, 1.0).astype(np.float32)


def _expand_map():
    pos = np.zeros((F, F), np.int32)
    pos[PAIR_A, PAIR_B] = np.arange(NPAIR)
    pos[PAIR_B, PAIR_A] = np.arange(NPAIR)
    rows = np.concatenate([np.arange(1 + F), 1 + F + pos.reshape(-1)]).astype(np.int32)
    outer = np.concatenate([np.zeros(1 + F, bool), np.ones(F * F, bool)])
    return rows, outer


EXPAND_ROWS, EXPAND_OUTER = _expand_map()


def shifted(value, axis, steps):
    count = lax.axis_size(axis)
    leading, last = (max(0, -steps), min(count, count - steps))
    return lax.ppermute(value, axis, [(source, source + steps) for source in range(leading, last)])


def norm_rows(values, gain):
    mean_sq = jnp.mean(values * values, axis=-1, keepdims=True)
    return values * lax.rsqrt(mean_sq + 1e-06) * gain.astype(jnp.float32)


def compact_features(heads_in, weighted):
    scaled = heads_in.astype(jnp.float32) * 0.5
    outer = scaled[..., PAIR_A] * scaled[..., PAIR_B]
    if weighted:
        outer = outer * PAIR_W
    ones = jnp.ones(scaled.shape[:-1] + (1,), jnp.float32)
    return jnp.concatenate([ones, scaled, outer], axis=-1)


def pair_weights(query, keys):
    score = jnp.einsum("nhf,mhf->hnm", query, keys, preferred_element_type=jnp.float32) * F ** (
        -0.5
    )
    return 1.0 + score + 0.5 * score * score


def on_device(
    tokens,
    prompt_lengths,
    norm_mixer,
    norm_conv,
    norm_mlp,
    w_query,
    w_key,
    w_value,
    w_out,
    w_proj,
    conv_kernel,
    w_gate,
    w_up,
    w_down,
):
    hp = lax.Precision.HIGHEST
    nrows = tokens.shape[0]
    heads = w_query.shape[1] // F
    nseq = lax.axis_size("seq")
    me = lax.axis_index("seq")
    my_start = me * nrows
    my_end = my_start + nrows
    place = my_start + jnp.arange(nrows, dtype=jnp.int32)
    ends = jnp.cumsum(prompt_lengths)
    below = ends[None, :] <= place[:, None]
    doc_start = jnp.max(jnp.where(below, ends[None, :], 0), axis=1)
    last_start = doc_start[-1]

    block_first = jnp.arange(nseq, dtype=jnp.int32) * nrows
    block_last_start = jnp.max(
        jnp.where(ends[None, :] <= block_first[:, None] + nrows - 1, ends[None, :], 0), axis=1
    )
    flags = block_last_start < block_first
    flags_pad = jnp.concatenate([jnp.zeros((nseq,), bool), flags])
    slot = jnp.arange(2 * nseq, dtype=jnp.int32)

    resid = tokens.astype(jnp.float32)
    n1 = norm_rows(resid, norm_mixer).astype(jnp.bfloat16)
    query = (
        jnp.dot(n1, w_query, preferred_element_type=jnp.float32)
        .astype(jnp.bfloat16)
        .reshape(nrows, heads, F)
    )
    keys = (
        jnp.dot(n1, w_key, preferred_element_type=jnp.float32)
        .astype(jnp.bfloat16)
        .reshape(nrows, heads, F)
    )
    values = (
        jnp.dot(n1, w_value, preferred_element_type=jnp.float32)
        .astype(jnp.bfloat16)
        .reshape(nrows, heads, DV)
    )
    values_f = values.astype(jnp.float32)

    tail = (place >= last_start).astype(jnp.float32)
    phik = compact_features(keys, False) * tail[:, None, None]
    v_aug = jnp.concatenate([values_f, jnp.ones((nrows, heads, 1), jnp.float32)], axis=-1)
    local_state = jnp.einsum("nhe,nhd->hed", phik, v_aug, precision=hp)

    window = shifted(local_state, "seq", 1)
    width = 1
    while width < nseq:
        inside = (slot >= me + nseq - width) & (slot < me + nseq)
        through = jnp.all(jnp.where(inside, flags_pad, True)).astype(jnp.float32)
        window = window + through * shifted(window, "seq", width)
        width *= 2
    carried = window

    local_mask = (place[None, :] <= place[:, None]) & (place[None, :] >= doc_start[:, None])
    weight_matrix = pair_weights(query, keys) * local_mask.astype(jnp.float32)[None]
    numerator_term = jnp.einsum("hnm,mhd->nhd", weight_matrix, values_f, precision=hp)
    denom = jnp.sum(weight_matrix, axis=2).T

    apply = (doc_start < my_start).astype(jnp.float32)
    phiq = compact_features(query, True)
    cross = jnp.einsum("nhe,hed->nhd", phiq, carried, precision=hp) * apply[:, None, None]
    numerator_term = numerator_term + cross[..., :DV]
    denom = denom + cross[..., DV]

    own_flag = flags[me].astype(jnp.float32)
    total = local_state + own_flag * carried
    full = jnp.take(total, EXPAND_ROWS, axis=1)
    full = jnp.where(EXPAND_OUTER[None, :, None], full / jnp.sqrt(jnp.float32(2.0)), full)
    count = (my_end - last_start).astype(jnp.float32)
    cache_state = (full[..., :DV] / count)[None]
    cache_norm = (full[..., DV] / count)[None]

    attn = (numerator_term / denom[:, :, None]).astype(jnp.bfloat16).reshape(nrows, heads * DV)
    mixed = lax.psum(
        jnp.dot(attn, w_out, preferred_element_type=jnp.float32).astype(jnp.bfloat16), "mp"
    ).astype(jnp.float32)
    res1 = resid + mixed
    n2 = norm_rows(res1, norm_conv).astype(jnp.bfloat16)
    width = w_proj.shape[1]
    own = lax.dynamic_slice_in_dim(n2, lax.axis_index("mp") * width, width, 1)
    proj = jnp.dot(n2, w_proj, preferred_element_type=jnp.float32)
    rim = shifted(own[nrows - (KC - 1) :], "seq", 1)
    extended = jnp.concatenate([rim, own], axis=0).astype(jnp.float32)
    conv = jnp.zeros((nrows, width), jnp.float32)
    for tap in range(KC):
        keep = (place - tap >= doc_start).astype(jnp.float32)
        conv = (
            conv
            + conv_kernel[tap].astype(jnp.float32)[None, :]
            * extended[KC - 1 - tap : KC - 1 - tap + nrows]
            * keep[:, None]
        )
    gated = (proj * conv).astype(jnp.bfloat16)
    gathered = lax.all_gather(gated, "mp", axis=1, tiled=True)
    res2 = res1 + gathered.astype(jnp.float32)
    n3 = norm_rows(res2, norm_mlp).astype(jnp.bfloat16)
    gate = jnp.dot(n3, w_gate, preferred_element_type=jnp.float32)
    upper = jnp.dot(n3, w_up, preferred_element_type=jnp.float32)
    hid = (jax.nn.silu(gate) * upper).astype(jnp.bfloat16)
    down = lax.psum(
        jnp.dot(hid, w_down, preferred_element_type=jnp.float32).astype(jnp.bfloat16), "mp"
    ).astype(jnp.float32)
    hidden_out = (res2 + down).astype(jnp.bfloat16)
    return (hidden_out, cache_state, cache_norm)


def solution(mesh):
    return jax.shard_map(
        on_device,
        mesh=mesh,
        in_specs=(
            P("seq", None),
            P(),
            P(),
            P(),
            P(),
            P(None, "mp"),
            P(None, "mp"),
            P(None, "mp"),
            P("mp", None),
            P(None, "mp"),
            P(None, "mp"),
            P(None, "mp"),
            P(None, "mp"),
            P("mp", None),
        ),
        out_specs=(P("seq", None), P("seq", "mp", None, None), P("seq", "mp", None)),
        check_vma=False,
    )
```

```python
import jax
import jax.numpy as jnp
import numpy as np
from jax import lax
from jax.sharding import PartitionSpec as P

F = 16
DV = 112
KC = 3
FEAT = 273

PAIR_A, PAIR_B = np.triu_indices(F)
NPAIR = PAIR_A.shape[0]
NCOMP = 1 + F + NPAIR
PAIR_W = np.where(PAIR_A == PAIR_B, 0.5, 1.0).astype(np.float32)


def _feature_maps():
    left = np.zeros((F, NCOMP), np.float32)
    right = np.zeros((F, NCOMP), np.float32)
    left_bias = np.zeros((NCOMP,), np.float32)
    right_bias = np.zeros((NCOMP,), np.float32)
    left_bias[0] = right_bias[0] = 1.0
    for a in range(F):
        left[a, 1 + a] = 1.0
        right_bias[1 + a] = 1.0
    left[PAIR_A, 1 + F + np.arange(NPAIR)] = 1.0
    right[PAIR_B, 1 + F + np.arange(NPAIR)] = 1.0
    right_q = right.copy()
    right_q[PAIR_B, 1 + F + np.arange(NPAIR)] = PAIR_W
    pos = np.zeros((F, F), np.int32)
    pos[PAIR_A, PAIR_B] = np.arange(NPAIR)
    pos[PAIR_B, PAIR_A] = np.arange(NPAIR)
    rows = np.concatenate([np.arange(1 + F), 1 + F + pos.reshape(-1)])
    select = np.zeros((FEAT, NCOMP), np.float32)
    select[np.arange(FEAT), rows] = 1.0
    outer = np.concatenate([np.zeros(1 + F, bool), np.ones(F * F, bool)])
    return left, right, right_q, left_bias, right_bias, select, outer


LEFT, RIGHT, RIGHT_Q, LEFT_BIAS, RIGHT_BIAS, SELECT, EXPAND_OUTER = _feature_maps()


def shifted(value, axis, steps):
    count = lax.axis_size(axis)
    leading, last = (max(0, -steps), min(count, count - steps))
    return lax.ppermute(value, axis, [(source, source + steps) for source in range(leading, last)])


def norm_rows(values, gain):
    mean_sq = jnp.mean(values * values, axis=-1, keepdims=True)
    return values * lax.rsqrt(mean_sq + 1e-06) * gain.astype(jnp.float32)


def compact_features(heads_in, weighted):
    scaled = heads_in * jnp.bfloat16(0.5)
    right = RIGHT_Q if weighted else RIGHT
    lhs = jnp.einsum("nhf,fe->nhe", scaled, jnp.asarray(LEFT, jnp.bfloat16), preferred_element_type=jnp.float32)
    rhs = jnp.einsum("nhf,fe->nhe", scaled, jnp.asarray(right, jnp.bfloat16), preferred_element_type=jnp.float32)
    return (lhs + LEFT_BIAS) * (rhs + RIGHT_BIAS)


def reduce_rows(x):
    n = lax.axis_size("mp")
    parts = lax.all_to_all(x.reshape((n, -1) + x.shape[1:]), "mp", 0, 0, tiled=False)
    return jnp.sum(parts.astype(jnp.float32), axis=0)


def gather_stack(c):
    n = lax.axis_size("mp")
    return lax.all_to_all(jnp.broadcast_to(c[None], (n,) + c.shape), "mp", 0, 0, tiled=False)


def own_rows(x):
    n = lax.axis_size("mp")
    rows = x.shape[0] // n
    return lax.dynamic_slice_in_dim(x, lax.axis_index("mp") * rows, rows, 0)


def pair_weights(query, keys):
    score = jnp.einsum("nhf,mhf->hnm", query, keys, preferred_element_type=jnp.float32) * F ** (
        -0.5
    )
    return 1.0 + score + 0.5 * score * score


def on_device(
    tokens,
    prompt_lengths,
    norm_mixer,
    norm_conv,
    norm_mlp,
    w_query,
    w_key,
    w_value,
    w_out,
    w_proj,
    conv_kernel,
    w_gate,
    w_up,
    w_down,
):
    hp = lax.Precision.HIGHEST
    nrows = tokens.shape[0]
    heads = w_query.shape[1] // F
    nseq = lax.axis_size("seq")
    me = lax.axis_index("seq")
    my_start = me * nrows
    my_end = my_start + nrows
    place = my_start + jnp.arange(nrows, dtype=jnp.int32)
    ends = jnp.cumsum(prompt_lengths)
    below = ends[None, :] <= place[:, None]
    doc_start = jnp.max(jnp.where(below, ends[None, :], 0), axis=1)
    last_start = doc_start[-1]

    block_first = jnp.arange(nseq, dtype=jnp.int32) * nrows
    block_last_start = jnp.max(
        jnp.where(ends[None, :] <= block_first[:, None] + nrows - 1, ends[None, :], 0), axis=1
    )
    flags = block_last_start < block_first
    flags_pad = jnp.concatenate([jnp.zeros((nseq,), bool), flags])
    slot = jnp.arange(2 * nseq, dtype=jnp.int32)

    resid = tokens.astype(jnp.float32)
    n1 = norm_rows(resid, norm_mixer).astype(jnp.bfloat16)
    query = (
        jnp.dot(n1, w_query, preferred_element_type=jnp.float32)
        .astype(jnp.bfloat16)
        .reshape(nrows, heads, F)
    )
    keys = (
        jnp.dot(n1, w_key, preferred_element_type=jnp.float32)
        .astype(jnp.bfloat16)
        .reshape(nrows, heads, F)
    )
    values = (
        jnp.dot(n1, w_value, preferred_element_type=jnp.float32)
        .astype(jnp.bfloat16)
        .reshape(nrows, heads, DV)
    )
    values_f = values.astype(jnp.float32)

    tail = (place >= last_start).astype(jnp.float32)
    phik = compact_features(keys, False) * tail[:, None, None]
    v_aug = jnp.concatenate([values_f, jnp.ones((nrows, heads, 1), jnp.float32)], axis=-1)
    local_state = jnp.einsum("nhe,nhd->hed", phik, v_aug, precision=hp)

    window = shifted(local_state, "seq", 1)
    width = 1
    while width < nseq:
        inside = (slot >= me + nseq - width) & (slot < me + nseq)
        through = jnp.all(jnp.where(inside, flags_pad, True)).astype(jnp.float32)
        window = window + through * shifted(window, "seq", width)
        width *= 2
    carried = window

    local_mask = (place[None, :] <= place[:, None]) & (place[None, :] >= doc_start[:, None])
    weight_matrix = pair_weights(query, keys) * local_mask.astype(jnp.float32)[None]
    numerator_term = jnp.einsum("hnm,mhd->nhd", weight_matrix, values_f, precision=hp)
    denom = jnp.sum(weight_matrix, axis=2).T

    apply = (doc_start < my_start).astype(jnp.float32)
    phiq = compact_features(query, True)
    cross = jnp.einsum("nhe,hed->nhd", phiq, carried, precision=hp) * apply[:, None, None]
    numerator_term = numerator_term + cross[..., :DV]
    denom = denom + cross[..., DV]

    own_flag = flags[me].astype(jnp.float32)
    total = local_state + own_flag * carried
    full = jnp.einsum("re,hed->hrd", SELECT, total, precision=hp)
    full = jnp.where(EXPAND_OUTER[None, :, None], full / jnp.sqrt(jnp.float32(2.0)), full)
    count = (my_end - last_start).astype(jnp.float32)
    cache_state = (full[..., :DV] / count)[None]
    cache_norm = (full[..., DV] / count)[None]

    attn = (numerator_term / denom[:, :, None]).astype(jnp.bfloat16).reshape(nrows, heads * DV)
    mixed_terms = jnp.dot(attn, w_out, preferred_element_type=jnp.float32).astype(jnp.bfloat16)
    mixed_rows = reduce_rows(mixed_terms).astype(jnp.bfloat16)
    mixed = gather_stack(mixed_rows).reshape(nrows, -1).astype(jnp.float32)
    res1 = resid + mixed
    n2 = norm_rows(res1, norm_conv).astype(jnp.bfloat16)
    width = w_proj.shape[1]
    own = lax.dynamic_slice_in_dim(n2, lax.axis_index("mp") * width, width, 1)
    proj = jnp.dot(n2, w_proj, preferred_element_type=jnp.float32)
    rim = shifted(own[nrows - (KC - 1) :], "seq", 1)
    extended = jnp.concatenate([rim, own], axis=0).astype(jnp.float32)
    conv = jnp.zeros((nrows, width), jnp.float32)
    for tap in range(KC):
        keep = (place - tap >= doc_start).astype(jnp.float32)
        conv = (
            conv
            + conv_kernel[tap].astype(jnp.float32)[None, :]
            * extended[KC - 1 - tap : KC - 1 - tap + nrows]
            * keep[:, None]
        )
    gated = (proj * conv).astype(jnp.bfloat16)
    gathered = gather_stack(gated).transpose(1, 0, 2).reshape(nrows, -1)
    res2 = res1 + gathered.astype(jnp.float32)
    n3 = norm_rows(res2, norm_mlp).astype(jnp.bfloat16)
    gate = jnp.dot(n3, w_gate, preferred_element_type=jnp.float32)
    upper = jnp.dot(n3, w_up, preferred_element_type=jnp.float32)
    hid = (jax.nn.silu(gate) * upper).astype(jnp.bfloat16)
    down_terms = jnp.dot(hid, w_down, preferred_element_type=jnp.float32).astype(jnp.bfloat16)
    out_rows = (own_rows(res2) + reduce_rows(down_terms)).astype(jnp.bfloat16)
    hidden_out = gather_stack(out_rows).reshape(nrows, -1)
    return (hidden_out, cache_state, cache_norm)


def solution(mesh):
    return jax.shard_map(
        on_device,
        mesh=mesh,
        in_specs=(
            P("seq", None),
            P(),
            P(),
            P(),
            P(),
            P(None, "mp"),
            P(None, "mp"),
            P(None, "mp"),
            P("mp", None),
            P(None, "mp"),
            P(None, "mp"),
            P(None, "mp"),
            P(None, "mp"),
            P("mp", None),
        ),
        out_specs=(P("seq", None), P("seq", "mp", None, None), P("seq", "mp", None)),
        check_vma=False,
    )
```

```python
import jax
import jax.numpy as jnp
import numpy as np
from jax import lax
from jax.sharding import PartitionSpec as P

F = 16
DV = 112
KC = 3
FEAT = 273

PAIR_A, PAIR_B = np.triu_indices(F)
NPAIR = PAIR_A.shape[0]
NCOMP = 1 + F + NPAIR
PAIR_W = np.where(PAIR_A == PAIR_B, 0.5, 1.0).astype(np.float32)


def _feature_maps():
    left = np.zeros((F, NCOMP), np.float32)
    right = np.zeros((F, NCOMP), np.float32)
    left_bias = np.zeros((NCOMP,), np.float32)
    right_bias = np.zeros((NCOMP,), np.float32)
    left_bias[0] = right_bias[0] = 1.0
    for a in range(F):
        left[a, 1 + a] = 1.0
        right_bias[1 + a] = 1.0
    left[PAIR_A, 1 + F + np.arange(NPAIR)] = 1.0
    right[PAIR_B, 1 + F + np.arange(NPAIR)] = 1.0
    right_q = right.copy()
    right_q[PAIR_B, 1 + F + np.arange(NPAIR)] = PAIR_W
    pos = np.zeros((F, F), np.int32)
    pos[PAIR_A, PAIR_B] = np.arange(NPAIR)
    pos[PAIR_B, PAIR_A] = np.arange(NPAIR)
    rows = np.concatenate([np.arange(1 + F), 1 + F + pos.reshape(-1)])
    select = np.zeros((FEAT, NCOMP), np.float32)
    select[np.arange(FEAT), rows] = 1.0
    outer = np.concatenate([np.zeros(1 + F, bool), np.ones(F * F, bool)])
    return left, right, right_q, left_bias, right_bias, select, outer


LEFT, RIGHT, RIGHT_Q, LEFT_BIAS, RIGHT_BIAS, SELECT, EXPAND_OUTER = _feature_maps()


def shifted(value, axis, steps):
    count = lax.axis_size(axis)
    leading, last = (max(0, -steps), min(count, count - steps))
    return lax.ppermute(value, axis, [(source, source + steps) for source in range(leading, last)])


def norm_rows(values, gain):
    mean_sq = jnp.mean(values * values, axis=-1, keepdims=True)
    return values * lax.rsqrt(mean_sq + 1e-06) * gain.astype(jnp.float32)


def compact_features(heads_in, weighted):
    scaled = heads_in * jnp.bfloat16(0.5)
    right = RIGHT_Q if weighted else RIGHT
    lhs = jnp.einsum("nhf,fe->nhe", scaled, jnp.asarray(LEFT, jnp.bfloat16), preferred_element_type=jnp.float32)
    rhs = jnp.einsum("nhf,fe->nhe", scaled, jnp.asarray(right, jnp.bfloat16), preferred_element_type=jnp.float32)
    return (lhs + LEFT_BIAS) * (rhs + RIGHT_BIAS)


def reduce_rows(x):
    n = lax.axis_size("mp")
    parts = lax.all_to_all(x.reshape((n, -1) + x.shape[1:]), "mp", 0, 0, tiled=False)
    return jnp.sum(parts.astype(jnp.float32), axis=0)


def gather_stack(c):
    n = lax.axis_size("mp")
    return lax.all_to_all(jnp.broadcast_to(c[None], (n,) + c.shape), "mp", 0, 0, tiled=False)


def own_rows(x):
    n = lax.axis_size("mp")
    rows = x.shape[0] // n
    return lax.dynamic_slice_in_dim(x, lax.axis_index("mp") * rows, rows, 0)


def pair_weights(query, keys):
    score = jnp.einsum("nhf,mhf->hnm", query, keys, preferred_element_type=jnp.float32) * F ** (
        -0.5
    )
    return 1.0 + score + 0.5 * score * score


def on_device(
    tokens,
    prompt_lengths,
    norm_mixer,
    norm_conv,
    norm_mlp,
    w_query,
    w_key,
    w_value,
    w_out,
    w_proj,
    conv_kernel,
    w_gate,
    w_up,
    w_down,
):
    hp = lax.Precision.HIGHEST
    nrows = tokens.shape[0]
    heads = w_query.shape[1] // F
    nseq = lax.axis_size("seq")
    me = lax.axis_index("seq")
    my_start = me * nrows
    my_end = my_start + nrows
    place = my_start + jnp.arange(nrows, dtype=jnp.int32)
    ends = jnp.cumsum(prompt_lengths)
    below = ends[None, :] <= place[:, None]
    doc_start = jnp.max(jnp.where(below, ends[None, :], 0), axis=1)
    last_start = doc_start[-1]

    block_first = jnp.arange(nseq, dtype=jnp.int32) * nrows
    block_last_start = jnp.max(
        jnp.where(ends[None, :] <= block_first[:, None] + nrows - 1, ends[None, :], 0), axis=1
    )
    flags = block_last_start < block_first
    flags_pad = jnp.concatenate([jnp.zeros((nseq,), bool), flags])
    slot = jnp.arange(2 * nseq, dtype=jnp.int32)

    resid = tokens.astype(jnp.float32)
    n1 = norm_rows(resid, norm_mixer).astype(jnp.bfloat16)
    query = (
        jnp.dot(n1, w_query, preferred_element_type=jnp.float32)
        .astype(jnp.bfloat16)
        .reshape(nrows, heads, F)
    )
    keys = (
        jnp.dot(n1, w_key, preferred_element_type=jnp.float32)
        .astype(jnp.bfloat16)
        .reshape(nrows, heads, F)
    )
    values = (
        jnp.dot(n1, w_value, preferred_element_type=jnp.float32)
        .astype(jnp.bfloat16)
        .reshape(nrows, heads, DV)
    )
    values_f = values.astype(jnp.float32)

    tail = (place >= last_start).astype(jnp.float32)
    phik = compact_features(keys, False) * tail[:, None, None]
    v_aug = jnp.concatenate([values_f, jnp.ones((nrows, heads, 1), jnp.float32)], axis=-1)
    local_state = jnp.einsum("nhe,nhd->hed", phik, v_aug, precision=hp)

    window = shifted(local_state.astype(jnp.bfloat16), "seq", 1).astype(jnp.float32)
    width = 1
    while width < nseq:
        inside = (slot >= me + nseq - width) & (slot < me + nseq)
        through = jnp.all(jnp.where(inside, flags_pad, True)).astype(jnp.float32)
        arrived = shifted(window.astype(jnp.bfloat16), "seq", width).astype(jnp.float32)
        window = window + through * arrived
        width *= 2
    carried = window

    local_mask = (place[None, :] <= place[:, None]) & (place[None, :] >= doc_start[:, None])
    weight_matrix = pair_weights(query, keys) * local_mask.astype(jnp.float32)[None]
    numerator_term = jnp.einsum("hnm,mhd->nhd", weight_matrix, values_f, precision=hp)
    denom = jnp.sum(weight_matrix, axis=2).T

    apply = (doc_start < my_start).astype(jnp.float32)
    phiq = compact_features(query, True)
    cross = jnp.einsum("nhe,hed->nhd", phiq, carried, precision=hp) * apply[:, None, None]
    numerator_term = numerator_term + cross[..., :DV]
    denom = denom + cross[..., DV]

    own_flag = flags[me].astype(jnp.float32)
    total = local_state + own_flag * carried
    full = jnp.einsum("re,hed->hrd", SELECT, total, precision=hp)
    full = jnp.where(EXPAND_OUTER[None, :, None], full / jnp.sqrt(jnp.float32(2.0)), full)
    count = (my_end - last_start).astype(jnp.float32)
    cache_state = (full[..., :DV] / count)[None]
    cache_norm = (full[..., DV] / count)[None]

    attn = (numerator_term / denom[:, :, None]).astype(jnp.bfloat16).reshape(nrows, heads * DV)
    mixed_terms = jnp.dot(attn, w_out, preferred_element_type=jnp.float32).astype(jnp.bfloat16)
    mixed_rows = reduce_rows(mixed_terms).astype(jnp.bfloat16)
    mixed = gather_stack(mixed_rows).reshape(nrows, -1).astype(jnp.float32)
    res1 = resid + mixed
    n2 = norm_rows(res1, norm_conv).astype(jnp.bfloat16)
    width = w_proj.shape[1]
    own = lax.dynamic_slice_in_dim(n2, lax.axis_index("mp") * width, width, 1)
    proj = jnp.dot(n2, w_proj, preferred_element_type=jnp.float32)
    rim = shifted(own[nrows - (KC - 1) :], "seq", 1)
    extended = jnp.concatenate([rim, own], axis=0).astype(jnp.float32)
    conv = jnp.zeros((nrows, width), jnp.float32)
    for tap in range(KC):
        keep = (place - tap >= doc_start).astype(jnp.float32)
        conv = (
            conv
            + conv_kernel[tap].astype(jnp.float32)[None, :]
            * extended[KC - 1 - tap : KC - 1 - tap + nrows]
            * keep[:, None]
        )
    gated = (proj * conv).astype(jnp.bfloat16)
    gathered = gather_stack(gated).transpose(1, 0, 2).reshape(nrows, -1)
    res2 = res1 + gathered.astype(jnp.float32)
    n3 = norm_rows(res2, norm_mlp).astype(jnp.bfloat16)
    gate = jnp.dot(n3, w_gate, preferred_element_type=jnp.float32)
    upper = jnp.dot(n3, w_up, preferred_element_type=jnp.float32)
    hid = (jax.nn.silu(gate) * upper).astype(jnp.bfloat16)
    down_terms = jnp.dot(hid, w_down, preferred_element_type=jnp.float32).astype(jnp.bfloat16)
    out_rows = (own_rows(res2) + reduce_rows(down_terms)).astype(jnp.bfloat16)
    hidden_out = gather_stack(out_rows).reshape(nrows, -1)
    return (hidden_out, cache_state, cache_norm)


def solution(mesh):
    return jax.shard_map(
        on_device,
        mesh=mesh,
        in_specs=(
            P("seq", None),
            P(),
            P(),
            P(),
            P(),
            P(None, "mp"),
            P(None, "mp"),
            P(None, "mp"),
            P("mp", None),
            P(None, "mp"),
            P(None, "mp"),
            P(None, "mp"),
            P(None, "mp"),
            P("mp", None),
        ),
        out_specs=(P("seq", None), P("seq", "mp", None, None), P("seq", "mp", None)),
        check_vma=False,
    )
```

```python
import jax
import jax.numpy as jnp
import numpy as np
from jax import lax
from jax.sharding import PartitionSpec as P

F = 16
DV = 112
KC = 3
FEAT = 273

PAIR_A, PAIR_B = np.triu_indices(F)
NPAIR = PAIR_A.shape[0]
NCOMP = 1 + F + NPAIR
PAIR_W = np.where(PAIR_A == PAIR_B, 0.5, 1.0).astype(np.float32)


def _feature_maps():
    left = np.zeros((F, NCOMP), np.float32)
    right = np.zeros((F, NCOMP), np.float32)
    left_bias = np.zeros((NCOMP,), np.float32)
    right_bias = np.zeros((NCOMP,), np.float32)
    left_bias[0] = right_bias[0] = 1.0
    for a in range(F):
        left[a, 1 + a] = 1.0
        right_bias[1 + a] = 1.0
    left[PAIR_A, 1 + F + np.arange(NPAIR)] = 1.0
    right[PAIR_B, 1 + F + np.arange(NPAIR)] = 1.0
    right_q = right.copy()
    right_q[PAIR_B, 1 + F + np.arange(NPAIR)] = PAIR_W
    pos = np.zeros((F, F), np.int32)
    pos[PAIR_A, PAIR_B] = np.arange(NPAIR)
    pos[PAIR_B, PAIR_A] = np.arange(NPAIR)
    rows = np.concatenate([np.arange(1 + F), 1 + F + pos.reshape(-1)])
    select = np.zeros((FEAT, NCOMP), np.float32)
    select[np.arange(FEAT), rows] = 1.0
    outer = np.concatenate([np.zeros(1 + F, bool), np.ones(F * F, bool)])
    return left, right, right_q, left_bias, right_bias, select, outer


LEFT, RIGHT, RIGHT_Q, LEFT_BIAS, RIGHT_BIAS, SELECT, EXPAND_OUTER = _feature_maps()


def shifted(value, axis, steps):
    count = lax.axis_size(axis)
    leading, last = (max(0, -steps), min(count, count - steps))
    return lax.ppermute(value, axis, [(source, source + steps) for source in range(leading, last)])


def norm_rows(values, gain):
    mean_sq = jnp.mean(values * values, axis=-1, keepdims=True)
    return values * lax.rsqrt(mean_sq + 1e-06) * gain.astype(jnp.float32)


def compact_features(heads_in, weighted):
    scaled = heads_in * jnp.bfloat16(0.5)
    right = RIGHT_Q if weighted else RIGHT
    lhs = jnp.einsum("nhf,fe->nhe", scaled, jnp.asarray(LEFT, jnp.bfloat16), preferred_element_type=jnp.float32)
    rhs = jnp.einsum("nhf,fe->nhe", scaled, jnp.asarray(right, jnp.bfloat16), preferred_element_type=jnp.float32)
    return (lhs + LEFT_BIAS) * (rhs + RIGHT_BIAS)


def reduce_rows(x):
    n = lax.axis_size("mp")
    parts = lax.all_to_all(x.reshape((n, -1) + x.shape[1:]), "mp", 0, 0, tiled=False)
    return jnp.sum(parts.astype(jnp.float32), axis=0)


def gather_stack(c):
    n = lax.axis_size("mp")
    return lax.all_to_all(jnp.broadcast_to(c[None], (n,) + c.shape), "mp", 0, 0, tiled=False)


def own_rows(x):
    n = lax.axis_size("mp")
    rows = x.shape[0] // n
    return lax.dynamic_slice_in_dim(x, lax.axis_index("mp") * rows, rows, 0)


def pair_weights(query, keys):
    score = jnp.einsum("nhf,mhf->hnm", query, keys, preferred_element_type=jnp.float32) * F ** (
        -0.5
    )
    return 1.0 + score + 0.5 * score * score


def on_device(
    tokens,
    prompt_lengths,
    norm_mixer,
    norm_conv,
    norm_mlp,
    w_query,
    w_key,
    w_value,
    w_out,
    w_proj,
    conv_kernel,
    w_gate,
    w_up,
    w_down,
):
    hp = lax.Precision.HIGHEST
    nrows = tokens.shape[0]
    heads = w_query.shape[1] // F
    nseq = lax.axis_size("seq")
    me = lax.axis_index("seq")
    my_start = me * nrows
    my_end = my_start + nrows
    place = my_start + jnp.arange(nrows, dtype=jnp.int32)
    ends = jnp.cumsum(prompt_lengths)
    below = ends[None, :] <= place[:, None]
    doc_start = jnp.max(jnp.where(below, ends[None, :], 0), axis=1)
    last_start = doc_start[-1]

    block_first = jnp.arange(nseq, dtype=jnp.int32) * nrows
    block_last_start = jnp.max(
        jnp.where(ends[None, :] <= block_first[:, None] + nrows - 1, ends[None, :], 0), axis=1
    )
    flags = block_last_start < block_first

    resid = tokens.astype(jnp.float32)
    n1 = norm_rows(resid, norm_mixer).astype(jnp.bfloat16)
    query = (
        jnp.dot(n1, w_query, preferred_element_type=jnp.float32)
        .astype(jnp.bfloat16)
        .reshape(nrows, heads, F)
    )
    keys = (
        jnp.dot(n1, w_key, preferred_element_type=jnp.float32)
        .astype(jnp.bfloat16)
        .reshape(nrows, heads, F)
    )
    values = (
        jnp.dot(n1, w_value, preferred_element_type=jnp.float32)
        .astype(jnp.bfloat16)
        .reshape(nrows, heads, DV)
    )
    values_f = values.astype(jnp.float32)

    tail = (place >= last_start).astype(jnp.float32)
    phik = compact_features(keys, False) * tail[:, None, None]
    v_aug = jnp.concatenate([values_f, jnp.ones((nrows, heads, 1), jnp.float32)], axis=-1)
    local_state = jnp.einsum("nhe,nhd->hed", phik, v_aug, precision=hp)

    payload = local_state.astype(jnp.bfloat16)
    everyone = lax.all_to_all(
        jnp.broadcast_to(payload[None], (nseq,) + payload.shape), "seq", 0, 0, tiled=False
    )
    breaks = jnp.cumsum((~flags).astype(jnp.int32))
    block = jnp.arange(nseq, dtype=jnp.int32)
    breaks_before_me = breaks[jnp.maximum(me - 1, 0)]
    coef = (block < me) & (breaks_before_me == breaks)
    carried = jnp.einsum(
        "s,shed->hed", coef.astype(jnp.bfloat16), everyone, preferred_element_type=jnp.float32
    )

    local_mask = (place[None, :] <= place[:, None]) & (place[None, :] >= doc_start[:, None])
    weight_matrix = pair_weights(query, keys) * local_mask.astype(jnp.float32)[None]
    numerator_term = jnp.einsum("hnm,mhd->nhd", weight_matrix, values_f, precision=hp)
    denom = jnp.sum(weight_matrix, axis=2).T

    apply = (doc_start < my_start).astype(jnp.float32)
    phiq = compact_features(query, True)
    cross = jnp.einsum("nhe,hed->nhd", phiq, carried, precision=hp) * apply[:, None, None]
    numerator_term = numerator_term + cross[..., :DV]
    denom = denom + cross[..., DV]

    own_flag = flags[me].astype(jnp.float32)
    total = local_state + own_flag * carried
    full = jnp.einsum("re,hed->hrd", SELECT, total, precision=hp)
    full = jnp.where(EXPAND_OUTER[None, :, None], full / jnp.sqrt(jnp.float32(2.0)), full)
    count = (my_end - last_start).astype(jnp.float32)
    cache_state = (full[..., :DV] / count)[None]
    cache_norm = (full[..., DV] / count)[None]

    attn = (numerator_term / denom[:, :, None]).astype(jnp.bfloat16).reshape(nrows, heads * DV)
    mixed_terms = jnp.dot(attn, w_out, preferred_element_type=jnp.float32).astype(jnp.bfloat16)
    mixed_rows = reduce_rows(mixed_terms).astype(jnp.bfloat16)
    mixed = gather_stack(mixed_rows).reshape(nrows, -1).astype(jnp.float32)
    res1 = resid + mixed
    n2 = norm_rows(res1, norm_conv).astype(jnp.bfloat16)
    width = w_proj.shape[1]
    own = lax.dynamic_slice_in_dim(n2, lax.axis_index("mp") * width, width, 1)
    proj = jnp.dot(n2, w_proj, preferred_element_type=jnp.float32)
    rim = shifted(own[nrows - (KC - 1) :], "seq", 1)
    extended = jnp.concatenate([rim, own], axis=0).astype(jnp.float32)
    conv = jnp.zeros((nrows, width), jnp.float32)
    for tap in range(KC):
        keep = (place - tap >= doc_start).astype(jnp.float32)
        conv = (
            conv
            + conv_kernel[tap].astype(jnp.float32)[None, :]
            * extended[KC - 1 - tap : KC - 1 - tap + nrows]
            * keep[:, None]
        )
    gated = (proj * conv).astype(jnp.bfloat16)
    gathered = gather_stack(gated).transpose(1, 0, 2).reshape(nrows, -1)
    res2 = res1 + gathered.astype(jnp.float32)
    n3 = norm_rows(res2, norm_mlp).astype(jnp.bfloat16)
    gate = jnp.dot(n3, w_gate, preferred_element_type=jnp.float32)
    upper = jnp.dot(n3, w_up, preferred_element_type=jnp.float32)
    hid = (jax.nn.silu(gate) * upper).astype(jnp.bfloat16)
    down_terms = jnp.dot(hid, w_down, preferred_element_type=jnp.float32).astype(jnp.bfloat16)
    out_rows = (own_rows(res2) + reduce_rows(down_terms)).astype(jnp.bfloat16)
    hidden_out = gather_stack(out_rows).reshape(nrows, -1)
    return (hidden_out, cache_state, cache_norm)


def solution(mesh):
    return jax.shard_map(
        on_device,
        mesh=mesh,
        in_specs=(
            P("seq", None),
            P(),
            P(),
            P(),
            P(),
            P(None, "mp"),
            P(None, "mp"),
            P(None, "mp"),
            P("mp", None),
            P(None, "mp"),
            P(None, "mp"),
            P(None, "mp"),
            P(None, "mp"),
            P("mp", None),
        ),
        out_specs=(P("seq", None), P("seq", "mp", None, None), P("seq", "mp", None)),
        check_vma=False,
    )
```

```python
import jax
import jax.numpy as jnp
import numpy as np
from jax import lax
from jax.sharding import PartitionSpec as P

F = 16
DV = 112
KC = 3
FEAT = 273

PAIR_A, PAIR_B = np.triu_indices(F)
NPAIR = PAIR_A.shape[0]
NCOMP = 1 + F + NPAIR
PAIR_W = np.where(PAIR_A == PAIR_B, 0.5, 1.0).astype(np.float32)


def _feature_maps():
    left = np.zeros((F, NCOMP), np.float32)
    right = np.zeros((F, NCOMP), np.float32)
    left_bias = np.zeros((NCOMP,), np.float32)
    right_bias = np.zeros((NCOMP,), np.float32)
    left_bias[0] = right_bias[0] = 1.0
    for a in range(F):
        left[a, 1 + a] = 1.0
        right_bias[1 + a] = 1.0
    left[PAIR_A, 1 + F + np.arange(NPAIR)] = 1.0
    right[PAIR_B, 1 + F + np.arange(NPAIR)] = 1.0
    right_q = right.copy()
    right_q[PAIR_B, 1 + F + np.arange(NPAIR)] = PAIR_W
    pos = np.zeros((F, F), np.int32)
    pos[PAIR_A, PAIR_B] = np.arange(NPAIR)
    pos[PAIR_B, PAIR_A] = np.arange(NPAIR)
    rows = np.concatenate([np.arange(1 + F), 1 + F + pos.reshape(-1)])
    select = np.zeros((FEAT, NCOMP), np.float32)
    select[np.arange(FEAT), rows] = 1.0
    outer = np.concatenate([np.zeros(1 + F, bool), np.ones(F * F, bool)])
    return left, right, right_q, left_bias, right_bias, select, outer


LEFT, RIGHT, RIGHT_Q, LEFT_BIAS, RIGHT_BIAS, SELECT, EXPAND_OUTER = _feature_maps()


def shifted(value, axis, steps):
    count = lax.axis_size(axis)
    leading, last = (max(0, -steps), min(count, count - steps))
    return lax.ppermute(value, axis, [(source, source + steps) for source in range(leading, last)])


def norm_rows(values, gain):
    mean_sq = jnp.mean(values * values, axis=-1, keepdims=True)
    return values * lax.rsqrt(mean_sq + 1e-06) * gain.astype(jnp.float32)


def compact_features(heads_in, weighted):
    scaled = heads_in * jnp.bfloat16(0.5)
    right = RIGHT_Q if weighted else RIGHT
    lhs = jnp.einsum("nhf,fe->nhe", scaled, jnp.asarray(LEFT, jnp.bfloat16), preferred_element_type=jnp.float32)
    rhs = jnp.einsum("nhf,fe->nhe", scaled, jnp.asarray(right, jnp.bfloat16), preferred_element_type=jnp.float32)
    return (lhs + LEFT_BIAS) * (rhs + RIGHT_BIAS)


def reduce_rows(x):
    n = lax.axis_size("mp")
    parts = lax.all_to_all(x.reshape((n, -1) + x.shape[1:]), "mp", 0, 0, tiled=False)
    return jnp.sum(parts.astype(jnp.float32), axis=0)


def gather_stack(c):
    n = lax.axis_size("mp")
    return lax.all_to_all(jnp.broadcast_to(c[None], (n,) + c.shape), "mp", 0, 0, tiled=False)


def own_rows(x):
    n = lax.axis_size("mp")
    rows = x.shape[0] // n
    return lax.dynamic_slice_in_dim(x, lax.axis_index("mp") * rows, rows, 0)


def pair_weights(query, keys):
    score = jnp.einsum("nhf,mhf->hnm", query, keys, preferred_element_type=jnp.float32) * F ** (
        -0.5
    )
    return 1.0 + score + 0.5 * score * score


def on_device(
    tokens,
    prompt_lengths,
    norm_mixer,
    norm_conv,
    norm_mlp,
    w_query,
    w_key,
    w_value,
    w_out,
    w_proj,
    conv_kernel,
    w_gate,
    w_up,
    w_down,
):
    hp = lax.Precision.HIGHEST
    nrows = tokens.shape[0]
    heads = w_query.shape[1] // F
    nseq = lax.axis_size("seq")
    me = lax.axis_index("seq")
    my_start = me * nrows
    my_end = my_start + nrows
    place = my_start + jnp.arange(nrows, dtype=jnp.int32)
    ends = jnp.cumsum(prompt_lengths)
    below = ends[None, :] <= place[:, None]
    doc_start = jnp.max(jnp.where(below, ends[None, :], 0), axis=1)
    last_start = doc_start[-1]

    block_first = jnp.arange(nseq, dtype=jnp.int32) * nrows
    block_last_start = jnp.max(
        jnp.where(ends[None, :] <= block_first[:, None] + nrows - 1, ends[None, :], 0), axis=1
    )
    flags = block_last_start < block_first

    resid = tokens.astype(jnp.float32)
    n1 = norm_rows(resid, norm_mixer).astype(jnp.bfloat16)
    query = (
        jnp.dot(n1, w_query, preferred_element_type=jnp.float32)
        .astype(jnp.bfloat16)
        .reshape(nrows, heads, F)
    )
    keys = (
        jnp.dot(n1, w_key, preferred_element_type=jnp.float32)
        .astype(jnp.bfloat16)
        .reshape(nrows, heads, F)
    )
    values = (
        jnp.dot(n1, w_value, preferred_element_type=jnp.float32)
        .astype(jnp.bfloat16)
        .reshape(nrows, heads, DV)
    )
    values_f = values.astype(jnp.float32)

    tail = (place >= last_start).astype(jnp.float32)
    phik = compact_features(keys, False) * tail[:, None, None]
    v_aug = jnp.concatenate([values_f, jnp.ones((nrows, heads, 1), jnp.float32)], axis=-1)
    local_state = jnp.einsum("nhe,nhd->hed", phik, v_aug, precision=hp)

    breaks = jnp.cumsum((~flags).astype(jnp.int32))

    def breaks_at(i):
        return jnp.where(i >= 0, breaks[jnp.maximum(i, 0)], 0)

    def through(w):
        return (breaks_at(me - 1) == breaks_at(me - w - 1)).astype(jnp.float32)

    def gather_window(piece, size, steps):
        total = piece
        for step in range(1, steps):
            arrived = shifted(piece.astype(jnp.bfloat16), "seq", step * size).astype(jnp.float32)
            total = total + through(step * size) * arrived
        return total

    first = [
        shifted(local_state.astype(jnp.bfloat16), "seq", i).astype(jnp.float32) for i in range(1, 5)
    ]
    window = first[0]
    for i in range(1, 4):
        window = window + through(i) * first[i]
    window = gather_window(window, 4, 4)
    window = gather_window(window, 16, 2)
    carried = window

    local_mask = (place[None, :] <= place[:, None]) & (place[None, :] >= doc_start[:, None])
    weight_matrix = pair_weights(query, keys) * local_mask.astype(jnp.float32)[None]
    numerator_term = jnp.einsum("hnm,mhd->nhd", weight_matrix, values_f, precision=hp)
    denom = jnp.sum(weight_matrix, axis=2).T

    apply = (doc_start < my_start).astype(jnp.float32)
    phiq = compact_features(query, True)
    cross = jnp.einsum("nhe,hed->nhd", phiq, carried, precision=hp) * apply[:, None, None]
    numerator_term = numerator_term + cross[..., :DV]
    denom = denom + cross[..., DV]

    own_flag = flags[me].astype(jnp.float32)
    total = local_state + own_flag * carried
    full = jnp.einsum("re,hed->hrd", SELECT, total, precision=hp)
    full = jnp.where(EXPAND_OUTER[None, :, None], full / jnp.sqrt(jnp.float32(2.0)), full)
    count = (my_end - last_start).astype(jnp.float32)
    cache_state = (full[..., :DV] / count)[None]
    cache_norm = (full[..., DV] / count)[None]

    attn = (numerator_term / denom[:, :, None]).astype(jnp.bfloat16).reshape(nrows, heads * DV)
    mixed_terms = jnp.dot(attn, w_out, preferred_element_type=jnp.float32).astype(jnp.bfloat16)
    mixed_rows = reduce_rows(mixed_terms).astype(jnp.bfloat16)
    mixed = gather_stack(mixed_rows).reshape(nrows, -1).astype(jnp.float32)
    res1 = resid + mixed
    n2 = norm_rows(res1, norm_conv).astype(jnp.bfloat16)
    width = w_proj.shape[1]
    own = lax.dynamic_slice_in_dim(n2, lax.axis_index("mp") * width, width, 1)
    proj = jnp.dot(n2, w_proj, preferred_element_type=jnp.float32)
    rim = shifted(own[nrows - (KC - 1) :], "seq", 1)
    extended = jnp.concatenate([rim, own], axis=0).astype(jnp.float32)
    conv = jnp.zeros((nrows, width), jnp.float32)
    for tap in range(KC):
        keep = (place - tap >= doc_start).astype(jnp.float32)
        conv = (
            conv
            + conv_kernel[tap].astype(jnp.float32)[None, :]
            * extended[KC - 1 - tap : KC - 1 - tap + nrows]
            * keep[:, None]
        )
    gated = (proj * conv).astype(jnp.bfloat16)
    gathered = gather_stack(gated).transpose(1, 0, 2).reshape(nrows, -1)
    res2 = res1 + gathered.astype(jnp.float32)
    n3 = norm_rows(res2, norm_mlp).astype(jnp.bfloat16)
    gate = jnp.dot(n3, w_gate, preferred_element_type=jnp.float32)
    upper = jnp.dot(n3, w_up, preferred_element_type=jnp.float32)
    hid = (jax.nn.silu(gate) * upper).astype(jnp.bfloat16)
    down_terms = jnp.dot(hid, w_down, preferred_element_type=jnp.float32).astype(jnp.bfloat16)
    out_rows = (own_rows(res2) + reduce_rows(down_terms)).astype(jnp.bfloat16)
    hidden_out = gather_stack(out_rows).reshape(nrows, -1)
    return (hidden_out, cache_state, cache_norm)


def solution(mesh):
    return jax.shard_map(
        on_device,
        mesh=mesh,
        in_specs=(
            P("seq", None),
            P(),
            P(),
            P(),
            P(),
            P(None, "mp"),
            P(None, "mp"),
            P(None, "mp"),
            P("mp", None),
            P(None, "mp"),
            P(None, "mp"),
            P(None, "mp"),
            P(None, "mp"),
            P("mp", None),
        ),
        out_specs=(P("seq", None), P("seq", "mp", None, None), P("seq", "mp", None)),
        check_vma=False,
    )
```

```python
import jax
import jax.numpy as jnp
import numpy as np
from jax import lax
from jax.sharding import PartitionSpec as P

F = 16
DV = 112
KC = 3
FEAT = 273
MP = ("y", "core")

PAIR_A, PAIR_B = np.triu_indices(F)
NPAIR = PAIR_A.shape[0]
NCOMP = 1 + F + NPAIR
PAIR_W = np.where(PAIR_A == PAIR_B, 0.5, 1.0).astype(np.float32)


def _feature_maps():
    left = np.zeros((F, NCOMP), np.float32)
    right = np.zeros((F, NCOMP), np.float32)
    left_bias = np.zeros((NCOMP,), np.float32)
    right_bias = np.zeros((NCOMP,), np.float32)
    left_bias[0] = right_bias[0] = 1.0
    for a in range(F):
        left[a, 1 + a] = 1.0
        right_bias[1 + a] = 1.0
    left[PAIR_A, 1 + F + np.arange(NPAIR)] = 1.0
    right[PAIR_B, 1 + F + np.arange(NPAIR)] = 1.0
    right_q = right.copy()
    right_q[PAIR_B, 1 + F + np.arange(NPAIR)] = PAIR_W
    pos = np.zeros((F, F), np.int32)
    pos[PAIR_A, PAIR_B] = np.arange(NPAIR)
    pos[PAIR_B, PAIR_A] = np.arange(NPAIR)
    rows = np.concatenate([np.arange(1 + F), 1 + F + pos.reshape(-1)])
    select = np.zeros((FEAT, NCOMP), np.float32)
    select[np.arange(FEAT), rows] = 1.0
    outer = np.concatenate([np.zeros(1 + F, bool), np.ones(F * F, bool)])
    return left, right, right_q, left_bias, right_bias, select, outer


LEFT, RIGHT, RIGHT_Q, LEFT_BIAS, RIGHT_BIAS, SELECT, EXPAND_OUTER = _feature_maps()


def shifted(value, axis, steps):
    count = lax.axis_size(axis)
    leading, last = (max(0, -steps), min(count, count - steps))
    return lax.ppermute(value, axis, [(source, source + steps) for source in range(leading, last)])


def norm_rows(values, gain):
    mean_sq = jnp.mean(values * values, axis=-1, keepdims=True)
    return values * lax.rsqrt(mean_sq + 1e-06) * gain.astype(jnp.float32)


def compact_features(heads_in, weighted):
    scaled = heads_in * jnp.bfloat16(0.5)
    right = RIGHT_Q if weighted else RIGHT
    lhs = jnp.einsum("nhf,fe->nhe", scaled, jnp.asarray(LEFT, jnp.bfloat16), preferred_element_type=jnp.float32)
    rhs = jnp.einsum("nhf,fe->nhe", scaled, jnp.asarray(right, jnp.bfloat16), preferred_element_type=jnp.float32)
    return (lhs + LEFT_BIAS) * (rhs + RIGHT_BIAS)


def reduce_rows(x):
    core = lax.axis_index("core")
    ny = lax.axis_size("y")
    chunks = x.reshape((ny, 2, -1) + x.shape[1:])
    mine = lax.dynamic_index_in_dim(chunks, core, 1, keepdims=False)
    theirs = lax.dynamic_index_in_dim(chunks, 1 - core, 1, keepdims=False)
    got = lax.ppermute(theirs, "core", [(0, 1), (1, 0)])
    pair = (mine.astype(jnp.float32) + got.astype(jnp.float32)).astype(jnp.bfloat16)
    parts = lax.all_to_all(pair, "y", 0, 0, tiled=False)
    return jnp.sum(parts.astype(jnp.float32), axis=0)


def gather_stack(c):
    core = lax.axis_index("core")
    ny = lax.axis_size("y")
    same = lax.all_to_all(jnp.broadcast_to(c[None], (ny,) + c.shape), "y", 0, 0, tiled=False)
    other = lax.ppermute(same, "core", [(0, 1), (1, 0)])
    low = jnp.where(core == 0, same, other)
    high = jnp.where(core == 0, other, same)
    return jnp.stack([low, high], axis=1).reshape((2 * ny,) + c.shape)


def own_rows(x):
    n = lax.axis_size(MP)
    rows = x.shape[0] // n
    return lax.dynamic_slice_in_dim(x, lax.axis_index(MP) * rows, rows, 0)


def pair_weights(query, keys):
    score = jnp.einsum("nhf,mhf->hnm", query, keys, preferred_element_type=jnp.float32) * F ** (
        -0.5
    )
    return 1.0 + score + 0.5 * score * score


def on_device(
    tokens,
    prompt_lengths,
    norm_mixer,
    norm_conv,
    norm_mlp,
    w_query,
    w_key,
    w_value,
    w_out,
    w_proj,
    conv_kernel,
    w_gate,
    w_up,
    w_down,
):
    hp = lax.Precision.HIGHEST
    nrows = tokens.shape[0]
    heads = w_query.shape[1] // F
    nseq = lax.axis_size("seq")
    me = lax.axis_index("seq")
    my_start = me * nrows
    my_end = my_start + nrows
    place = my_start + jnp.arange(nrows, dtype=jnp.int32)
    ends = jnp.cumsum(prompt_lengths)
    below = ends[None, :] <= place[:, None]
    doc_start = jnp.max(jnp.where(below, ends[None, :], 0), axis=1)
    last_start = doc_start[-1]

    block_first = jnp.arange(nseq, dtype=jnp.int32) * nrows
    block_last_start = jnp.max(
        jnp.where(ends[None, :] <= block_first[:, None] + nrows - 1, ends[None, :], 0), axis=1
    )
    flags = block_last_start < block_first

    resid = tokens.astype(jnp.float32)
    n1 = norm_rows(resid, norm_mixer).astype(jnp.bfloat16)
    query = (
        jnp.dot(n1, w_query, preferred_element_type=jnp.float32)
        .astype(jnp.bfloat16)
        .reshape(nrows, heads, F)
    )
    keys = (
        jnp.dot(n1, w_key, preferred_element_type=jnp.float32)
        .astype(jnp.bfloat16)
        .reshape(nrows, heads, F)
    )
    values = (
        jnp.dot(n1, w_value, preferred_element_type=jnp.float32)
        .astype(jnp.bfloat16)
        .reshape(nrows, heads, DV)
    )
    values_f = values.astype(jnp.float32)

    tail = (place >= last_start).astype(jnp.float32)
    phik = compact_features(keys, False) * tail[:, None, None]
    v_aug = jnp.concatenate([values_f, jnp.ones((nrows, heads, 1), jnp.float32)], axis=-1)
    local_state = jnp.einsum("nhe,nhd->hed", phik, v_aug, precision=hp)

    breaks = jnp.cumsum((~flags).astype(jnp.int32))

    def breaks_at(i):
        return jnp.where(i >= 0, breaks[jnp.maximum(i, 0)], 0)

    def through(w):
        return (breaks_at(me - 1) == breaks_at(me - w - 1)).astype(jnp.float32)

    def gather_window(piece, size, steps):
        total = piece
        for step in range(1, steps):
            arrived = shifted(piece.astype(jnp.bfloat16), "seq", step * size).astype(jnp.float32)
            total = total + through(step * size) * arrived
        return total

    first = [
        shifted(local_state.astype(jnp.bfloat16), "seq", i).astype(jnp.float32) for i in range(1, 5)
    ]
    window = first[0]
    for i in range(1, 4):
        window = window + through(i) * first[i]
    window = gather_window(window, 4, 4)
    window = gather_window(window, 16, 2)
    carried = window

    local_mask = (place[None, :] <= place[:, None]) & (place[None, :] >= doc_start[:, None])
    weight_matrix = pair_weights(query, keys) * local_mask.astype(jnp.float32)[None]
    numerator_term = jnp.einsum("hnm,mhd->nhd", weight_matrix, values_f, precision=hp)
    denom = jnp.sum(weight_matrix, axis=2).T

    apply = (doc_start < my_start).astype(jnp.float32)
    phiq = compact_features(query, True)
    cross = jnp.einsum("nhe,hed->nhd", phiq, carried, precision=hp) * apply[:, None, None]
    numerator_term = numerator_term + cross[..., :DV]
    denom = denom + cross[..., DV]

    own_flag = flags[me].astype(jnp.float32)
    total = local_state + own_flag * carried
    full = jnp.einsum("re,hed->hrd", SELECT, total, precision=hp)
    full = jnp.where(EXPAND_OUTER[None, :, None], full / jnp.sqrt(jnp.float32(2.0)), full)
    count = (my_end - last_start).astype(jnp.float32)
    cache_state = (full[..., :DV] / count)[None]
    cache_norm = (full[..., DV] / count)[None]

    attn = (numerator_term / denom[:, :, None]).astype(jnp.bfloat16).reshape(nrows, heads * DV)
    mixed_terms = jnp.dot(attn, w_out, preferred_element_type=jnp.float32).astype(jnp.bfloat16)
    mixed_rows = reduce_rows(mixed_terms).astype(jnp.bfloat16)
    mixed = gather_stack(mixed_rows).reshape(nrows, -1).astype(jnp.float32)
    res1 = resid + mixed
    n2 = norm_rows(res1, norm_conv).astype(jnp.bfloat16)
    width = w_proj.shape[1]
    own = lax.dynamic_slice_in_dim(n2, lax.axis_index(MP) * width, width, 1)
    proj = jnp.dot(n2, w_proj, preferred_element_type=jnp.float32)
    rim = shifted(own[nrows - (KC - 1) :], "seq", 1)
    extended = jnp.concatenate([rim, own], axis=0).astype(jnp.float32)
    conv = jnp.zeros((nrows, width), jnp.float32)
    for tap in range(KC):
        keep = (place - tap >= doc_start).astype(jnp.float32)
        conv = (
            conv
            + conv_kernel[tap].astype(jnp.float32)[None, :]
            * extended[KC - 1 - tap : KC - 1 - tap + nrows]
            * keep[:, None]
        )
    gated = (proj * conv).astype(jnp.bfloat16)
    gathered = gather_stack(gated).transpose(1, 0, 2).reshape(nrows, -1)
    res2 = res1 + gathered.astype(jnp.float32)
    n3 = norm_rows(res2, norm_mlp).astype(jnp.bfloat16)
    gate = jnp.dot(n3, w_gate, preferred_element_type=jnp.float32)
    upper = jnp.dot(n3, w_up, preferred_element_type=jnp.float32)
    hid = (jax.nn.silu(gate) * upper).astype(jnp.bfloat16)
    down_terms = jnp.dot(hid, w_down, preferred_element_type=jnp.float32).astype(jnp.bfloat16)
    out_rows = (own_rows(res2) + reduce_rows(down_terms)).astype(jnp.bfloat16)
    hidden_out = gather_stack(out_rows).reshape(nrows, -1)
    return (hidden_out, cache_state, cache_norm)


def solution(mesh):
    nseq, nmp = mesh.devices.shape
    split = jax.sharding.Mesh(mesh.devices.reshape(nseq, nmp // 2, 2), ("seq", "y", "core"))
    return jax.shard_map(
        on_device,
        mesh=split,
        in_specs=(
            P("seq", None),
            P(),
            P(),
            P(),
            P(),
            P(None, MP),
            P(None, MP),
            P(None, MP),
            P(MP, None),
            P(None, MP),
            P(None, MP),
            P(None, MP),
            P(None, MP),
            P(MP, None),
        ),
        out_specs=(P("seq", None), P("seq", MP, None, None), P("seq", MP, None)),
        check_vma=False,
    )
```

```python
import jax
import jax.numpy as jnp
import numpy as np
from jax import lax
from jax.sharding import PartitionSpec as P

F = 16
DV = 112
KC = 3
FEAT = 273
MP = ("y", "core")
SEQ = ("x", "z")

PAIR_A, PAIR_B = np.triu_indices(F)
NPAIR = PAIR_A.shape[0]
NCOMP = 1 + F + NPAIR
PAIR_W = np.where(PAIR_A == PAIR_B, 0.5, 1.0).astype(np.float32)


def _feature_maps():
    left = np.zeros((F, NCOMP), np.float32)
    right = np.zeros((F, NCOMP), np.float32)
    left_bias = np.zeros((NCOMP,), np.float32)
    right_bias = np.zeros((NCOMP,), np.float32)
    left_bias[0] = right_bias[0] = 1.0
    for a in range(F):
        left[a, 1 + a] = 1.0
        right_bias[1 + a] = 1.0
    left[PAIR_A, 1 + F + np.arange(NPAIR)] = 1.0
    right[PAIR_B, 1 + F + np.arange(NPAIR)] = 1.0
    right_q = right.copy()
    right_q[PAIR_B, 1 + F + np.arange(NPAIR)] = PAIR_W
    pos = np.zeros((F, F), np.int32)
    pos[PAIR_A, PAIR_B] = np.arange(NPAIR)
    pos[PAIR_B, PAIR_A] = np.arange(NPAIR)
    rows = np.concatenate([np.arange(1 + F), 1 + F + pos.reshape(-1)])
    select = np.zeros((FEAT, NCOMP), np.float32)
    select[np.arange(FEAT), rows] = 1.0
    outer = np.concatenate([np.zeros(1 + F, bool), np.ones(F * F, bool)])
    return left, right, right_q, left_bias, right_bias, select, outer


LEFT, RIGHT, RIGHT_Q, LEFT_BIAS, RIGHT_BIAS, SELECT, EXPAND_OUTER = _feature_maps()


def shifted(value, axis, steps):
    count = lax.axis_size(axis)
    leading, last = (max(0, -steps), min(count, count - steps))
    return lax.ppermute(value, axis, [(source, source + steps) for source in range(leading, last)])


def norm_rows(values, gain):
    mean_sq = jnp.mean(values * values, axis=-1, keepdims=True)
    return values * lax.rsqrt(mean_sq + 1e-06) * gain.astype(jnp.float32)


def compact_features(heads_in, weighted):
    scaled = heads_in * jnp.bfloat16(0.5)
    right = RIGHT_Q if weighted else RIGHT
    lhs = jnp.einsum("nhf,fe->nhe", scaled, jnp.asarray(LEFT, jnp.bfloat16), preferred_element_type=jnp.float32)
    rhs = jnp.einsum("nhf,fe->nhe", scaled, jnp.asarray(right, jnp.bfloat16), preferred_element_type=jnp.float32)
    return (lhs + LEFT_BIAS) * (rhs + RIGHT_BIAS)


def reduce_rows(x):
    core = lax.axis_index("core")
    ny = lax.axis_size("y")
    chunks = x.reshape((ny, 2, -1) + x.shape[1:])
    mine = lax.dynamic_index_in_dim(chunks, core, 1, keepdims=False)
    theirs = lax.dynamic_index_in_dim(chunks, 1 - core, 1, keepdims=False)
    got = lax.ppermute(theirs, "core", [(0, 1), (1, 0)])
    pair = (mine.astype(jnp.float32) + got.astype(jnp.float32)).astype(jnp.bfloat16)
    parts = lax.all_to_all(pair, "y", 0, 0, tiled=False)
    return jnp.sum(parts.astype(jnp.float32), axis=0)


def gather_stack(c):
    core = lax.axis_index("core")
    ny = lax.axis_size("y")
    same = lax.all_to_all(jnp.broadcast_to(c[None], (ny,) + c.shape), "y", 0, 0, tiled=False)
    other = lax.ppermute(same, "core", [(0, 1), (1, 0)])
    low = jnp.where(core == 0, same, other)
    high = jnp.where(core == 0, other, same)
    return jnp.stack([low, high], axis=1).reshape((2 * ny,) + c.shape)


def own_rows(x):
    n = lax.axis_size(MP)
    rows = x.shape[0] // n
    return lax.dynamic_slice_in_dim(x, lax.axis_index(MP) * rows, rows, 0)


def pair_weights(query, keys):
    score = jnp.einsum("nhf,mhf->hnm", query, keys, preferred_element_type=jnp.float32) * F ** (
        -0.5
    )
    return 1.0 + score + 0.5 * score * score


def on_device(
    tokens,
    prompt_lengths,
    norm_mixer,
    norm_conv,
    norm_mlp,
    w_query,
    w_key,
    w_value,
    w_out,
    w_proj,
    conv_kernel,
    w_gate,
    w_up,
    w_down,
):
    hp = lax.Precision.HIGHEST
    nrows = tokens.shape[0]
    heads = w_query.shape[1] // F
    nseq = lax.axis_size(SEQ)
    me = lax.axis_index(SEQ)
    my_start = me * nrows
    my_end = my_start + nrows
    place = my_start + jnp.arange(nrows, dtype=jnp.int32)
    ends = jnp.cumsum(prompt_lengths)
    below = ends[None, :] <= place[:, None]
    doc_start = jnp.max(jnp.where(below, ends[None, :], 0), axis=1)
    last_start = doc_start[-1]

    block_first = jnp.arange(nseq, dtype=jnp.int32) * nrows
    block_last_start = jnp.max(
        jnp.where(ends[None, :] <= block_first[:, None] + nrows - 1, ends[None, :], 0), axis=1
    )
    flags = block_last_start < block_first

    resid = tokens.astype(jnp.float32)
    n1 = norm_rows(resid, norm_mixer).astype(jnp.bfloat16)
    query = (
        jnp.dot(n1, w_query, preferred_element_type=jnp.float32)
        .astype(jnp.bfloat16)
        .reshape(nrows, heads, F)
    )
    keys = (
        jnp.dot(n1, w_key, preferred_element_type=jnp.float32)
        .astype(jnp.bfloat16)
        .reshape(nrows, heads, F)
    )
    values = (
        jnp.dot(n1, w_value, preferred_element_type=jnp.float32)
        .astype(jnp.bfloat16)
        .reshape(nrows, heads, DV)
    )
    values_f = values.astype(jnp.float32)

    tail = (place >= last_start).astype(jnp.float32)
    phik = compact_features(keys, False) * tail[:, None, None]
    v_aug = jnp.concatenate([values_f, jnp.ones((nrows, heads, 1), jnp.float32)], axis=-1)
    local_state = jnp.einsum("nhe,nhd->hed", phik, v_aug, precision=hp)

    breaks = jnp.cumsum((~flags).astype(jnp.int32))

    def breaks_at(i):
        return jnp.where(i >= 0, breaks[jnp.maximum(i, 0)], 0)

    def chain(upto, first_block, count, stride, stack):
        index = jnp.arange(count, dtype=jnp.int32)
        last_of = first_block + index * stride + stride - 1
        keep = (last_of <= upto) & (breaks_at(upto) == breaks_at(last_of))
        return jnp.einsum(
            "s,shed->hed", keep.astype(jnp.bfloat16), stack, preferred_element_type=jnp.float32
        )

    nz = lax.axis_size("z")
    nx = lax.axis_size("x")
    group = lax.axis_index("x")
    group_first = group * nz
    payload = local_state.astype(jnp.bfloat16)
    members = lax.all_to_all(jnp.broadcast_to(payload[None], (nz,) + payload.shape), "z", 0, 0, tiled=False)
    within = chain(me - 1, group_first, nz, 1, members)
    group_end = chain(group_first + nz - 1, group_first, nz, 1, members).astype(jnp.bfloat16)
    ends_all = lax.all_to_all(jnp.broadcast_to(group_end[None], (nx,) + group_end.shape), "x", 0, 0, tiled=False)
    carry_in = chain(group_first - 1, 0, nx, nz, ends_all)
    into_block = (breaks_at(me - 1) == breaks_at(group_first - 1)).astype(jnp.float32)
    carried = within + into_block * carry_in

    local_mask = (place[None, :] <= place[:, None]) & (place[None, :] >= doc_start[:, None])
    weight_matrix = pair_weights(query, keys) * local_mask.astype(jnp.float32)[None]
    numerator_term = jnp.einsum("hnm,mhd->nhd", weight_matrix, values_f, precision=hp)
    denom = jnp.sum(weight_matrix, axis=2).T

    apply = (doc_start < my_start).astype(jnp.float32)
    phiq = compact_features(query, True)
    cross = jnp.einsum("nhe,hed->nhd", phiq, carried, precision=hp) * apply[:, None, None]
    numerator_term = numerator_term + cross[..., :DV]
    denom = denom + cross[..., DV]

    own_flag = flags[me].astype(jnp.float32)
    total = local_state + own_flag * carried
    full = jnp.einsum("re,hed->hrd", SELECT, total, precision=hp)
    full = jnp.where(EXPAND_OUTER[None, :, None], full / jnp.sqrt(jnp.float32(2.0)), full)
    count = (my_end - last_start).astype(jnp.float32)
    cache_state = (full[..., :DV] / count)[None]
    cache_norm = (full[..., DV] / count)[None]

    attn = (numerator_term / denom[:, :, None]).astype(jnp.bfloat16).reshape(nrows, heads * DV)
    mixed_terms = jnp.dot(attn, w_out, preferred_element_type=jnp.float32).astype(jnp.bfloat16)
    mixed_rows = reduce_rows(mixed_terms).astype(jnp.bfloat16)
    mixed = gather_stack(mixed_rows).reshape(nrows, -1).astype(jnp.float32)
    res1 = resid + mixed
    n2 = norm_rows(res1, norm_conv).astype(jnp.bfloat16)
    width = w_proj.shape[1]
    own = lax.dynamic_slice_in_dim(n2, lax.axis_index(MP) * width, width, 1)
    proj = jnp.dot(n2, w_proj, preferred_element_type=jnp.float32)
    rim = shifted(own[nrows - (KC - 1) :], SEQ, 1)
    extended = jnp.concatenate([rim, own], axis=0).astype(jnp.float32)
    conv = jnp.zeros((nrows, width), jnp.float32)
    for tap in range(KC):
        keep = (place - tap >= doc_start).astype(jnp.float32)
        conv = (
            conv
            + conv_kernel[tap].astype(jnp.float32)[None, :]
            * extended[KC - 1 - tap : KC - 1 - tap + nrows]
            * keep[:, None]
        )
    gated = (proj * conv).astype(jnp.bfloat16)
    gathered = gather_stack(gated).transpose(1, 0, 2).reshape(nrows, -1)
    res2 = res1 + gathered.astype(jnp.float32)
    n3 = norm_rows(res2, norm_mlp).astype(jnp.bfloat16)
    gate = jnp.dot(n3, w_gate, preferred_element_type=jnp.float32)
    upper = jnp.dot(n3, w_up, preferred_element_type=jnp.float32)
    hid = (jax.nn.silu(gate) * upper).astype(jnp.bfloat16)
    down_terms = jnp.dot(hid, w_down, preferred_element_type=jnp.float32).astype(jnp.bfloat16)
    out_rows = (own_rows(res2) + reduce_rows(down_terms)).astype(jnp.bfloat16)
    hidden_out = gather_stack(out_rows).reshape(nrows, -1)
    return (hidden_out, cache_state, cache_norm)


def solution(mesh):
    nseq, nmp = mesh.devices.shape
    nx = 4 if nseq % 4 == 0 else 1
    split = jax.sharding.Mesh(
        mesh.devices.reshape(nx, nseq // nx, nmp // 2, 2), ("x", "z", "y", "core")
    )
    return jax.shard_map(
        on_device,
        mesh=split,
        in_specs=(
            P(SEQ, None),
            P(),
            P(),
            P(),
            P(),
            P(None, MP),
            P(None, MP),
            P(None, MP),
            P(MP, None),
            P(None, MP),
            P(None, MP),
            P(None, MP),
            P(None, MP),
            P(MP, None),
        ),
        out_specs=(P(SEQ, None), P(SEQ, MP, None, None), P(SEQ, MP, None)),
        check_vma=False,
    )
```

```python
import jax
import jax.numpy as jnp
import numpy as np
from jax import lax
from jax.sharding import PartitionSpec as P

F = 16
DV = 112
KC = 3
FEAT = 273
MP = ("y", "core")
SEQ = ("x", "z")

PAIR_A, PAIR_B = np.triu_indices(F)
NPAIR = PAIR_A.shape[0]
NCOMP = 1 + F + NPAIR
PAIR_W = np.where(PAIR_A == PAIR_B, 0.5, 1.0).astype(np.float32)


def _feature_maps():
    left = np.zeros((F, NCOMP), np.float32)
    right = np.zeros((F, NCOMP), np.float32)
    left_bias = np.zeros((NCOMP,), np.float32)
    right_bias = np.zeros((NCOMP,), np.float32)
    left_bias[0] = right_bias[0] = 1.0
    for a in range(F):
        left[a, 1 + a] = 1.0
        right_bias[1 + a] = 1.0
    left[PAIR_A, 1 + F + np.arange(NPAIR)] = 1.0
    right[PAIR_B, 1 + F + np.arange(NPAIR)] = 1.0
    right_q = right.copy()
    right_q[PAIR_B, 1 + F + np.arange(NPAIR)] = PAIR_W
    pos = np.zeros((F, F), np.int32)
    pos[PAIR_A, PAIR_B] = np.arange(NPAIR)
    pos[PAIR_B, PAIR_A] = np.arange(NPAIR)
    rows = np.concatenate([np.arange(1 + F), 1 + F + pos.reshape(-1)])
    select = np.zeros((FEAT, NCOMP), np.float32)
    select[np.arange(FEAT), rows] = 1.0
    outer = np.concatenate([np.zeros(1 + F, bool), np.ones(F * F, bool)])
    return left, right, right_q, left_bias, right_bias, select, outer


LEFT, RIGHT, RIGHT_Q, LEFT_BIAS, RIGHT_BIAS, SELECT, EXPAND_OUTER = _feature_maps()


def shifted(value, axis, steps):
    count = lax.axis_size(axis)
    leading, last = (max(0, -steps), min(count, count - steps))
    return lax.ppermute(value, axis, [(source, source + steps) for source in range(leading, last)])


def norm_rows(values, gain):
    mean_sq = jnp.mean(values * values, axis=-1, keepdims=True)
    return values * lax.rsqrt(mean_sq + 1e-06) * gain.astype(jnp.float32)


def compact_features(heads_in, weighted):
    scaled = heads_in * jnp.bfloat16(0.5)
    right = RIGHT_Q if weighted else RIGHT
    lhs = jnp.einsum("nhf,fe->nhe", scaled, jnp.asarray(LEFT, jnp.bfloat16), preferred_element_type=jnp.float32)
    rhs = jnp.einsum("nhf,fe->nhe", scaled, jnp.asarray(right, jnp.bfloat16), preferred_element_type=jnp.float32)
    return (lhs + LEFT_BIAS) * (rhs + RIGHT_BIAS)


def reduce_rows(x):
    core = lax.axis_index("core")
    ny = lax.axis_size("y")
    chunks = x.reshape((ny, 2, -1) + x.shape[1:])
    mine = lax.dynamic_index_in_dim(chunks, core, 1, keepdims=False)
    theirs = lax.dynamic_index_in_dim(chunks, 1 - core, 1, keepdims=False)
    got = lax.ppermute(theirs, "core", [(0, 1), (1, 0)])
    pair = (mine.astype(jnp.float32) + got.astype(jnp.float32)).astype(jnp.bfloat16)
    parts = lax.all_to_all(pair, "y", 0, 0, tiled=False)
    return jnp.sum(parts.astype(jnp.float32), axis=0)


def gather_stack(c):
    core = lax.axis_index("core")
    ny = lax.axis_size("y")
    same = lax.all_to_all(jnp.broadcast_to(c[None], (ny,) + c.shape), "y", 0, 0, tiled=False)
    other = lax.ppermute(same, "core", [(0, 1), (1, 0)])
    low = jnp.where(core == 0, same, other)
    high = jnp.where(core == 0, other, same)
    return jnp.stack([low, high], axis=1).reshape((2 * ny,) + c.shape)


def gather_columns(c):
    core = lax.axis_index("core")
    ny = lax.axis_size("y")
    spread = jnp.broadcast_to(c[:, None], (c.shape[0], ny) + c.shape[1:])
    same = lax.all_to_all(spread, "y", 1, 1, tiled=False)
    other = lax.ppermute(same, "core", [(0, 1), (1, 0)])
    low = jnp.where(core == 0, same, other)
    high = jnp.where(core == 0, other, same)
    return jnp.stack([low, high], axis=2).reshape(c.shape[0], -1)


def own_rows(x):
    n = lax.axis_size(MP)
    rows = x.shape[0] // n
    return lax.dynamic_slice_in_dim(x, lax.axis_index(MP) * rows, rows, 0)


def pair_weights(query, keys):
    score = jnp.einsum("nhf,mhf->hnm", query, keys, preferred_element_type=jnp.float32) * F ** (
        -0.5
    )
    return 1.0 + score + 0.5 * score * score


def on_device(
    tokens,
    prompt_lengths,
    norm_mixer,
    norm_conv,
    norm_mlp,
    w_query,
    w_key,
    w_value,
    w_out,
    w_proj,
    conv_kernel,
    w_gate,
    w_up,
    w_down,
):
    hp = lax.Precision.HIGHEST
    nrows = tokens.shape[0]
    heads = w_query.shape[1] // F
    nseq = lax.axis_size(SEQ)
    me = lax.axis_index(SEQ)
    my_start = me * nrows
    my_end = my_start + nrows
    place = my_start + jnp.arange(nrows, dtype=jnp.int32)
    ends = jnp.cumsum(prompt_lengths)
    below = ends[None, :] <= place[:, None]
    doc_start = jnp.max(jnp.where(below, ends[None, :], 0), axis=1)
    last_start = doc_start[-1]

    block_first = jnp.arange(nseq, dtype=jnp.int32) * nrows
    block_last_start = jnp.max(
        jnp.where(ends[None, :] <= block_first[:, None] + nrows - 1, ends[None, :], 0), axis=1
    )
    flags = block_last_start < block_first

    resid = tokens.astype(jnp.float32)
    n1 = norm_rows(resid, norm_mixer).astype(jnp.bfloat16)
    query = (
        jnp.dot(n1, w_query, preferred_element_type=jnp.float32)
        .astype(jnp.bfloat16)
        .reshape(nrows, heads, F)
    )
    keys = (
        jnp.dot(n1, w_key, preferred_element_type=jnp.float32)
        .astype(jnp.bfloat16)
        .reshape(nrows, heads, F)
    )
    values = (
        jnp.dot(n1, w_value, preferred_element_type=jnp.float32)
        .astype(jnp.bfloat16)
        .reshape(nrows, heads, DV)
    )
    values_f = values.astype(jnp.float32)

    tail = (place >= last_start).astype(jnp.float32)
    phik = compact_features(keys, False) * tail[:, None, None]
    v_aug = jnp.concatenate([values_f, jnp.ones((nrows, heads, 1), jnp.float32)], axis=-1)
    local_state = jnp.einsum("nhe,nhd->hed", phik, v_aug, precision=hp)

    breaks = jnp.cumsum((~flags).astype(jnp.int32))

    def breaks_at(i):
        return jnp.where(i >= 0, breaks[jnp.maximum(i, 0)], 0)

    def chain(upto, first_block, count, stride, stack):
        index = jnp.arange(count, dtype=jnp.int32)
        last_of = first_block + index * stride + stride - 1
        keep = (last_of <= upto) & (breaks_at(upto) == breaks_at(last_of))
        return jnp.einsum(
            "s,shed->hed", keep.astype(jnp.bfloat16), stack, preferred_element_type=jnp.float32
        )

    nz = lax.axis_size("z")
    nx = lax.axis_size("x")
    group = lax.axis_index("x")
    group_first = group * nz
    payload = local_state.astype(jnp.bfloat16)
    members = lax.all_to_all(jnp.broadcast_to(payload[None], (nz,) + payload.shape), "z", 0, 0, tiled=False)
    within = chain(me - 1, group_first, nz, 1, members)
    group_end = chain(group_first + nz - 1, group_first, nz, 1, members).astype(jnp.bfloat16)
    ends_all = lax.all_to_all(jnp.broadcast_to(group_end[None], (nx,) + group_end.shape), "x", 0, 0, tiled=False)
    carry_in = chain(group_first - 1, 0, nx, nz, ends_all)
    into_block = (breaks_at(me - 1) == breaks_at(group_first - 1)).astype(jnp.float32)
    carried = within + into_block * carry_in

    local_mask = (place[None, :] <= place[:, None]) & (place[None, :] >= doc_start[:, None])
    weight_matrix = pair_weights(query, keys) * local_mask.astype(jnp.float32)[None]
    numerator_term = jnp.einsum("hnm,mhd->nhd", weight_matrix, values_f, precision=hp)
    denom = jnp.sum(weight_matrix, axis=2).T

    apply = (doc_start < my_start).astype(jnp.float32)
    phiq = compact_features(query, True)
    cross = jnp.einsum("nhe,hed->nhd", phiq, carried, precision=hp) * apply[:, None, None]
    numerator_term = numerator_term + cross[..., :DV]
    denom = denom + cross[..., DV]

    own_flag = flags[me].astype(jnp.float32)
    total = local_state + own_flag * carried
    full = jnp.einsum("re,hed->hrd", SELECT, total, precision=hp)
    full = jnp.where(EXPAND_OUTER[None, :, None], full / jnp.sqrt(jnp.float32(2.0)), full)
    count = (my_end - last_start).astype(jnp.float32)
    cache_state = (full[..., :DV] / count)[None]
    cache_norm = (full[..., DV] / count)[None]

    attn = (numerator_term / denom[:, :, None]).astype(jnp.bfloat16).reshape(nrows, heads * DV)
    mixed_terms = jnp.dot(attn, w_out, preferred_element_type=jnp.float32).astype(jnp.bfloat16)
    mixed_rows = reduce_rows(mixed_terms).astype(jnp.bfloat16)
    mixed = gather_stack(mixed_rows).reshape(nrows, -1).astype(jnp.float32)
    res1 = resid + mixed
    n2 = norm_rows(res1, norm_conv).astype(jnp.bfloat16)
    width = w_proj.shape[1]
    own = lax.dynamic_slice_in_dim(n2, lax.axis_index(MP) * width, width, 1)
    proj = jnp.dot(n2, w_proj, preferred_element_type=jnp.float32)
    rim = shifted(own[nrows - (KC - 1) :], SEQ, 1)
    extended = jnp.concatenate([rim, own], axis=0).astype(jnp.float32)
    conv = jnp.zeros((nrows, width), jnp.float32)
    for tap in range(KC):
        keep = (place - tap >= doc_start).astype(jnp.float32)
        conv = (
            conv
            + conv_kernel[tap].astype(jnp.float32)[None, :]
            * extended[KC - 1 - tap : KC - 1 - tap + nrows]
            * keep[:, None]
        )
    gated = (proj * conv).astype(jnp.bfloat16)
    gathered = gather_columns(gated)
    res2 = res1 + gathered.astype(jnp.float32)
    n3 = norm_rows(res2, norm_mlp).astype(jnp.bfloat16)
    gate = jnp.dot(n3, w_gate, preferred_element_type=jnp.float32)
    upper = jnp.dot(n3, w_up, preferred_element_type=jnp.float32)
    hid = (jax.nn.silu(gate) * upper).astype(jnp.bfloat16)
    down_terms = jnp.dot(hid, w_down, preferred_element_type=jnp.float32).astype(jnp.bfloat16)
    res2_rows = (own_rows(resid) + own_rows(mixed)) + own_rows(gathered).astype(jnp.float32)
    out_rows = (res2_rows + reduce_rows(down_terms)).astype(jnp.bfloat16)
    hidden_out = gather_stack(out_rows).reshape(nrows, -1)
    return (hidden_out, cache_state, cache_norm)


def solution(mesh):
    nseq, nmp = mesh.devices.shape
    nx = 4 if nseq % 4 == 0 else 1
    split = jax.sharding.Mesh(
        mesh.devices.reshape(nx, nseq // nx, nmp // 2, 2), ("x", "z", "y", "core")
    )
    return jax.shard_map(
        on_device,
        mesh=split,
        in_specs=(
            P(SEQ, None),
            P(),
            P(),
            P(),
            P(),
            P(None, MP),
            P(None, MP),
            P(None, MP),
            P(MP, None),
            P(None, MP),
            P(None, MP),
            P(None, MP),
            P(None, MP),
            P(MP, None),
        ),
        out_specs=(P(SEQ, None), P(SEQ, MP, None, None), P(SEQ, MP, None)),
        check_vma=False,
    )
```

```python
import jax
import jax.numpy as jnp
import numpy as np
from jax import lax
from jax.sharding import PartitionSpec as P

F = 16
DV = 112
KC = 3
FEAT = 273
MP = ("y", "core")
SEQ = ("x", "z")

PAIR_A, PAIR_B = np.triu_indices(F)
NPAIR = PAIR_A.shape[0]
NCOMP = 1 + F + NPAIR
PAIR_W = np.where(PAIR_A == PAIR_B, 0.5, 1.0).astype(np.float32)


def _feature_maps():
    left = np.zeros((F, NCOMP), np.float32)
    right = np.zeros((F, NCOMP), np.float32)
    left_bias = np.zeros((NCOMP,), np.float32)
    right_bias = np.zeros((NCOMP,), np.float32)
    left_bias[0] = right_bias[0] = 1.0
    for a in range(F):
        left[a, 1 + a] = 1.0
        right_bias[1 + a] = 1.0
    left[PAIR_A, 1 + F + np.arange(NPAIR)] = 1.0
    right[PAIR_B, 1 + F + np.arange(NPAIR)] = 1.0
    right_q = right.copy()
    right_q[PAIR_B, 1 + F + np.arange(NPAIR)] = PAIR_W
    pos = np.zeros((F, F), np.int32)
    pos[PAIR_A, PAIR_B] = np.arange(NPAIR)
    pos[PAIR_B, PAIR_A] = np.arange(NPAIR)
    rows = np.concatenate([np.arange(1 + F), 1 + F + pos.reshape(-1)])
    select = np.zeros((FEAT, NCOMP), np.float32)
    select[np.arange(FEAT), rows] = 1.0
    outer = np.concatenate([np.zeros(1 + F, bool), np.ones(F * F, bool)])
    return left, right, right_q, left_bias, right_bias, select, outer


LEFT, RIGHT, RIGHT_Q, LEFT_BIAS, RIGHT_BIAS, SELECT, EXPAND_OUTER = _feature_maps()


def shifted(value, axis, steps):
    count = lax.axis_size(axis)
    leading, last = (max(0, -steps), min(count, count - steps))
    return lax.ppermute(value, axis, [(source, source + steps) for source in range(leading, last)])


def norm_rows(values, gain):
    mean_sq = jnp.mean(values * values, axis=-1, keepdims=True)
    return values * lax.rsqrt(mean_sq + 1e-06) * gain.astype(jnp.float32)


def compact_features(heads_in, weighted):
    scaled = heads_in * jnp.bfloat16(0.5)
    right = RIGHT_Q if weighted else RIGHT
    lhs = jnp.einsum("nhf,fe->nhe", scaled, jnp.asarray(LEFT, jnp.bfloat16), preferred_element_type=jnp.float32)
    rhs = jnp.einsum("nhf,fe->nhe", scaled, jnp.asarray(right, jnp.bfloat16), preferred_element_type=jnp.float32)
    return (lhs + LEFT_BIAS) * (rhs + RIGHT_BIAS)


def reduce_rows(x):
    core = lax.axis_index("core")
    ny = lax.axis_size("y")
    chunks = x.reshape((ny, 2, -1) + x.shape[1:])
    mine = lax.dynamic_index_in_dim(chunks, core, 1, keepdims=False)
    theirs = lax.dynamic_index_in_dim(chunks, 1 - core, 1, keepdims=False)
    got = lax.ppermute(theirs, "core", [(0, 1), (1, 0)])
    pair = (mine.astype(jnp.float32) + got.astype(jnp.float32)).astype(jnp.bfloat16)
    parts = lax.all_to_all(pair, "y", 0, 0, tiled=False)
    return jnp.sum(parts.astype(jnp.float32), axis=0)


def gather_stack(c):
    core = lax.axis_index("core")
    ny = lax.axis_size("y")
    same = lax.all_to_all(jnp.broadcast_to(c[None], (ny,) + c.shape), "y", 0, 0, tiled=False)
    other = lax.ppermute(same, "core", [(0, 1), (1, 0)])
    out = jnp.zeros((ny, 2) + c.shape, c.dtype)
    out = lax.dynamic_update_index_in_dim(out, same[:, None], core, 1)
    out = lax.dynamic_update_index_in_dim(out, other[:, None], 1 - core, 1)
    return out.reshape((2 * ny,) + c.shape)


def own_rows(x):
    n = lax.axis_size(MP)
    rows = x.shape[0] // n
    return lax.dynamic_slice_in_dim(x, lax.axis_index(MP) * rows, rows, 0)


def pair_weights(query, keys):
    score = jnp.einsum("nhf,mhf->hnm", query, keys, preferred_element_type=jnp.float32) * F ** (
        -0.5
    )
    return 1.0 + score + 0.5 * score * score


def on_device(
    tokens,
    prompt_lengths,
    norm_mixer,
    norm_conv,
    norm_mlp,
    w_query,
    w_key,
    w_value,
    w_out,
    w_proj,
    conv_kernel,
    w_gate,
    w_up,
    w_down,
):
    hp = lax.Precision.HIGHEST
    nrows = tokens.shape[0]
    heads = w_query.shape[1] // F
    nseq = lax.axis_size(SEQ)
    me = lax.axis_index(SEQ)
    my_start = me * nrows
    my_end = my_start + nrows
    place = my_start + jnp.arange(nrows, dtype=jnp.int32)
    ends = jnp.cumsum(prompt_lengths)
    below = ends[None, :] <= place[:, None]
    doc_start = jnp.max(jnp.where(below, ends[None, :], 0), axis=1)
    last_start = doc_start[-1]

    block_first = jnp.arange(nseq, dtype=jnp.int32) * nrows
    block_last_start = jnp.max(
        jnp.where(ends[None, :] <= block_first[:, None] + nrows - 1, ends[None, :], 0), axis=1
    )
    flags = block_last_start < block_first

    resid = tokens.astype(jnp.float32)
    n1 = norm_rows(resid, norm_mixer).astype(jnp.bfloat16)
    query = (
        jnp.dot(n1, w_query, preferred_element_type=jnp.float32)
        .astype(jnp.bfloat16)
        .reshape(nrows, heads, F)
    )
    keys = (
        jnp.dot(n1, w_key, preferred_element_type=jnp.float32)
        .astype(jnp.bfloat16)
        .reshape(nrows, heads, F)
    )
    values = (
        jnp.dot(n1, w_value, preferred_element_type=jnp.float32)
        .astype(jnp.bfloat16)
        .reshape(nrows, heads, DV)
    )
    values_f = values.astype(jnp.float32)

    tail = (place >= last_start).astype(jnp.float32)
    phik = compact_features(keys, False) * tail[:, None, None]
    v_aug = jnp.concatenate([values_f, jnp.ones((nrows, heads, 1), jnp.float32)], axis=-1)
    local_state = jnp.einsum("nhe,nhd->hed", phik, v_aug, precision=hp)

    breaks = jnp.cumsum((~flags).astype(jnp.int32))

    def breaks_at(i):
        return jnp.where(i >= 0, breaks[jnp.maximum(i, 0)], 0)

    def chain(upto, first_block, count, stride, stack):
        index = jnp.arange(count, dtype=jnp.int32)
        last_of = first_block + index * stride + stride - 1
        keep = (last_of <= upto) & (breaks_at(upto) == breaks_at(last_of))
        return jnp.einsum(
            "s,shed->hed", keep.astype(jnp.bfloat16), stack, preferred_element_type=jnp.float32
        )

    nz = lax.axis_size("z")
    nx = lax.axis_size("x")
    group = lax.axis_index("x")
    group_first = group * nz
    payload = local_state.astype(jnp.bfloat16)
    members = lax.all_to_all(jnp.broadcast_to(payload[None], (nz,) + payload.shape), "z", 0, 0, tiled=False)
    within = chain(me - 1, group_first, nz, 1, members)
    group_end = chain(group_first + nz - 1, group_first, nz, 1, members).astype(jnp.bfloat16)
    ends_all = lax.all_to_all(jnp.broadcast_to(group_end[None], (nx,) + group_end.shape), "x", 0, 0, tiled=False)
    carry_in = chain(group_first - 1, 0, nx, nz, ends_all)
    into_block = (breaks_at(me - 1) == breaks_at(group_first - 1)).astype(jnp.float32)
    carried = within + into_block * carry_in

    local_mask = (place[None, :] <= place[:, None]) & (place[None, :] >= doc_start[:, None])
    weight_matrix = pair_weights(query, keys) * local_mask.astype(jnp.float32)[None]
    numerator_term = jnp.einsum("hnm,mhd->nhd", weight_matrix, values_f, precision=hp)
    denom = jnp.sum(weight_matrix, axis=2).T

    apply = (doc_start < my_start).astype(jnp.float32)
    phiq = compact_features(query, True)
    cross = jnp.einsum("nhe,hed->nhd", phiq, carried, precision=hp) * apply[:, None, None]
    numerator_term = numerator_term + cross[..., :DV]
    denom = denom + cross[..., DV]

    own_flag = flags[me].astype(jnp.float32)
    total = local_state + own_flag * carried
    full = jnp.einsum("re,hed->hrd", SELECT, total, precision=hp)
    full = jnp.where(EXPAND_OUTER[None, :, None], full / jnp.sqrt(jnp.float32(2.0)), full)
    count = (my_end - last_start).astype(jnp.float32)
    cache_state = (full[..., :DV] / count)[None]
    cache_norm = (full[..., DV] / count)[None]

    attn = (numerator_term / denom[:, :, None]).astype(jnp.bfloat16).reshape(nrows, heads * DV)
    mixed_terms = jnp.dot(attn, w_out, preferred_element_type=jnp.float32).astype(jnp.bfloat16)
    mixed_rows = reduce_rows(mixed_terms).astype(jnp.bfloat16)
    mixed = gather_stack(mixed_rows).reshape(nrows, -1).astype(jnp.float32)
    res1 = resid + mixed
    n2 = norm_rows(res1, norm_conv).astype(jnp.bfloat16)
    width = w_proj.shape[1]
    own = lax.dynamic_slice_in_dim(n2, lax.axis_index(MP) * width, width, 1)
    proj = jnp.dot(n2, w_proj, preferred_element_type=jnp.float32)
    rim = shifted(own[nrows - (KC - 1) :], SEQ, 1)
    extended = jnp.concatenate([rim, own], axis=0).astype(jnp.float32)
    conv = jnp.zeros((nrows, width), jnp.float32)
    for tap in range(KC):
        keep = (place - tap >= doc_start).astype(jnp.float32)
        conv = (
            conv
            + conv_kernel[tap].astype(jnp.float32)[None, :]
            * extended[KC - 1 - tap : KC - 1 - tap + nrows]
            * keep[:, None]
        )
    gated = (proj * conv).astype(jnp.bfloat16)
    gathered = gather_stack(gated).transpose(1, 0, 2).reshape(nrows, -1)
    res2 = res1 + gathered.astype(jnp.float32)
    n3 = norm_rows(res2, norm_mlp).astype(jnp.bfloat16)
    gate = jnp.dot(n3, w_gate, preferred_element_type=jnp.float32)
    upper = jnp.dot(n3, w_up, preferred_element_type=jnp.float32)
    hid = (jax.nn.silu(gate) * upper).astype(jnp.bfloat16)
    down_terms = jnp.dot(hid, w_down, preferred_element_type=jnp.float32).astype(jnp.bfloat16)
    out_rows = (own_rows(res2) + reduce_rows(down_terms)).astype(jnp.bfloat16)
    hidden_out = gather_stack(out_rows).reshape(nrows, -1)
    return (hidden_out, cache_state, cache_norm)


def solution(mesh):
    nseq, nmp = mesh.devices.shape
    nx = 4 if nseq % 4 == 0 else 1
    split = jax.sharding.Mesh(
        mesh.devices.reshape(nx, nseq // nx, nmp // 2, 2), ("x", "z", "y", "core")
    )
    return jax.shard_map(
        on_device,
        mesh=split,
        in_specs=(
            P(SEQ, None),
            P(),
            P(),
            P(),
            P(),
            P(None, MP),
            P(None, MP),
            P(None, MP),
            P(MP, None),
            P(None, MP),
            P(None, MP),
            P(None, MP),
            P(None, MP),
            P(MP, None),
        ),
        out_specs=(P(SEQ, None), P(SEQ, MP, None, None), P(SEQ, MP, None)),
        check_vma=False,
    )
```

```python
import jax
import jax.numpy as jnp
import numpy as np
from jax import lax
from jax.sharding import PartitionSpec as P

F = 16
DV = 112
KC = 3
FEAT = 273
MP = ("y", "core")
SEQ = ("x", "z")

PAIR_A, PAIR_B = np.triu_indices(F)
NPAIR = PAIR_A.shape[0]
NCOMP = 1 + F + NPAIR
PAIR_W = np.where(PAIR_A == PAIR_B, 0.5, 1.0).astype(np.float32)


def _feature_maps():
    left = np.zeros((F, NCOMP), np.float32)
    right = np.zeros((F, NCOMP), np.float32)
    left_bias = np.zeros((NCOMP,), np.float32)
    right_bias = np.zeros((NCOMP,), np.float32)
    left_bias[0] = right_bias[0] = 1.0
    for a in range(F):
        left[a, 1 + a] = 1.0
        right_bias[1 + a] = 1.0
    left[PAIR_A, 1 + F + np.arange(NPAIR)] = 1.0
    right[PAIR_B, 1 + F + np.arange(NPAIR)] = 1.0
    right_q = right.copy()
    right_q[PAIR_B, 1 + F + np.arange(NPAIR)] = PAIR_W
    pos = np.zeros((F, F), np.int32)
    pos[PAIR_A, PAIR_B] = np.arange(NPAIR)
    pos[PAIR_B, PAIR_A] = np.arange(NPAIR)
    rows = np.concatenate([np.arange(1 + F), 1 + F + pos.reshape(-1)])
    select = np.zeros((FEAT, NCOMP), np.float32)
    select[np.arange(FEAT), rows] = 1.0
    outer = np.concatenate([np.zeros(1 + F, bool), np.ones(F * F, bool)])
    return left, right, right_q, left_bias, right_bias, select, outer


LEFT, RIGHT, RIGHT_Q, LEFT_BIAS, RIGHT_BIAS, SELECT, EXPAND_OUTER = _feature_maps()


def shifted(value, axis, steps):
    count = lax.axis_size(axis)
    leading, last = (max(0, -steps), min(count, count - steps))
    return lax.ppermute(value, axis, [(source, source + steps) for source in range(leading, last)])


def norm_rows(values, gain):
    mean_sq = jnp.mean(values * values, axis=-1, keepdims=True)
    return values * lax.rsqrt(mean_sq + 1e-06) * gain.astype(jnp.float32)


def compact_features(heads_in, weighted):
    scaled = heads_in * jnp.bfloat16(0.5)
    right = RIGHT_Q if weighted else RIGHT
    lhs = jnp.einsum("nhf,fe->nhe", scaled, jnp.asarray(LEFT, jnp.bfloat16), preferred_element_type=jnp.float32)
    rhs = jnp.einsum("nhf,fe->nhe", scaled, jnp.asarray(right, jnp.bfloat16), preferred_element_type=jnp.float32)
    return (lhs + LEFT_BIAS) * (rhs + RIGHT_BIAS)


def reduce_rows(x):
    core = lax.axis_index("core")
    ny = lax.axis_size("y")
    chunks = x.reshape((ny, 2, -1) + x.shape[1:])
    mine = lax.dynamic_index_in_dim(chunks, core, 1, keepdims=False)
    theirs = lax.dynamic_index_in_dim(chunks, 1 - core, 1, keepdims=False)
    got = lax.ppermute(theirs, "core", [(0, 1), (1, 0)])
    pair = (mine.astype(jnp.float32) + got.astype(jnp.float32)).astype(jnp.bfloat16)
    parts = lax.all_to_all(pair, "y", 0, 0, tiled=False)
    return jnp.sum(parts.astype(jnp.float32), axis=0)


def gather_stack(c):
    core = lax.axis_index("core")
    ny = lax.axis_size("y")
    same = lax.all_to_all(jnp.broadcast_to(c[None], (ny,) + c.shape), "y", 0, 0, tiled=False)
    other = lax.ppermute(same, "core", [(0, 1), (1, 0)])
    out = jnp.zeros((ny, 2) + c.shape, c.dtype)
    out = lax.dynamic_update_index_in_dim(out, same[:, None], core, 1)
    out = lax.dynamic_update_index_in_dim(out, other[:, None], 1 - core, 1)
    return out.reshape((2 * ny,) + c.shape)


def own_rows(x):
    n = lax.axis_size(MP)
    rows = x.shape[0] // n
    return lax.dynamic_slice_in_dim(x, lax.axis_index(MP) * rows, rows, 0)


def pair_weights(query, keys):
    score = jnp.einsum("nhf,mhf->hnm", query, keys, preferred_element_type=jnp.float32) * F ** (
        -0.5
    )
    return 1.0 + score + 0.5 * score * score


def on_device(
    tokens,
    prompt_lengths,
    norm_mixer,
    norm_conv,
    norm_mlp,
    w_query,
    w_key,
    w_value,
    w_out,
    w_proj,
    conv_kernel,
    w_gate,
    w_up,
    w_down,
):
    hp = lax.Precision.HIGHEST
    nrows = tokens.shape[0]
    heads = w_query.shape[1] // F
    nseq = lax.axis_size(SEQ)
    me = lax.axis_index(SEQ)
    my_start = me * nrows
    my_end = my_start + nrows
    place = my_start + jnp.arange(nrows, dtype=jnp.int32)
    ends = jnp.cumsum(prompt_lengths)
    below = ends[None, :] <= place[:, None]
    doc_start = jnp.max(jnp.where(below, ends[None, :], 0), axis=1)
    last_start = doc_start[-1]

    block_first = jnp.arange(nseq, dtype=jnp.int32) * nrows
    block_last_start = jnp.max(
        jnp.where(ends[None, :] <= block_first[:, None] + nrows - 1, ends[None, :], 0), axis=1
    )
    flags = block_last_start < block_first

    resid = tokens.astype(jnp.float32)
    n1 = norm_rows(resid, norm_mixer).astype(jnp.bfloat16)
    query = (
        jnp.dot(n1, w_query, preferred_element_type=jnp.float32)
        .astype(jnp.bfloat16)
        .reshape(nrows, heads, F)
    )
    keys = (
        jnp.dot(n1, w_key, preferred_element_type=jnp.float32)
        .astype(jnp.bfloat16)
        .reshape(nrows, heads, F)
    )
    values = (
        jnp.dot(n1, w_value, preferred_element_type=jnp.float32)
        .astype(jnp.bfloat16)
        .reshape(nrows, heads, DV)
    )
    values_f = values.astype(jnp.float32)

    tail = (place >= last_start).astype(jnp.float32)
    phik = compact_features(keys, False) * tail[:, None, None]
    v_aug = jnp.concatenate([values_f, jnp.ones((nrows, heads, 1), jnp.float32)], axis=-1)
    local_state = jnp.einsum("nhe,nhd->hed", phik, v_aug, precision=hp)

    breaks = jnp.cumsum((~flags).astype(jnp.int32))

    def breaks_at(i):
        return jnp.where(i >= 0, breaks[jnp.maximum(i, 0)], 0)

    def chain(upto, first_block, count, stride, stack):
        index = jnp.arange(count, dtype=jnp.int32)
        last_of = first_block + index * stride + stride - 1
        keep = (last_of <= upto) & (breaks_at(upto) == breaks_at(last_of))
        return jnp.einsum(
            "s,shed->hed", keep.astype(jnp.bfloat16), stack, preferred_element_type=jnp.float32
        )

    nz = lax.axis_size("z")
    nx = lax.axis_size("x")
    group = lax.axis_index("x")
    group_first = group * nz
    payload = local_state.astype(jnp.bfloat16)
    members = lax.all_to_all(jnp.broadcast_to(payload[None], (nz,) + payload.shape), "z", 0, 0, tiled=False)
    within = chain(me - 1, group_first, nz, 1, members)
    group_end = chain(group_first + nz - 1, group_first, nz, 1, members).astype(jnp.bfloat16)
    ends_all = lax.all_to_all(jnp.broadcast_to(group_end[None], (nx,) + group_end.shape), "x", 0, 0, tiled=False)
    carry_in = chain(group_first - 1, 0, nx, nz, ends_all)
    into_block = (breaks_at(me - 1) == breaks_at(group_first - 1)).astype(jnp.float32)
    carried = within + into_block * carry_in

    local_mask = (place[None, :] <= place[:, None]) & (place[None, :] >= doc_start[:, None])
    weight_matrix = pair_weights(query, keys) * local_mask.astype(jnp.float32)[None]
    numerator_term = jnp.einsum("hnm,mhd->nhd", weight_matrix, values_f, precision=hp)
    denom = jnp.sum(weight_matrix, axis=2).T

    apply = (doc_start < my_start).astype(jnp.float32)
    phiq = compact_features(query, True)
    cross = jnp.einsum("nhe,hed->nhd", phiq, carried, precision=hp) * apply[:, None, None]
    numerator_term = numerator_term + cross[..., :DV]
    denom = denom + cross[..., DV]

    own_flag = flags[me].astype(jnp.float32)
    total = local_state + own_flag * carried
    full = jnp.einsum("re,hed->hrd", SELECT, total, precision=hp)
    full = jnp.where(EXPAND_OUTER[None, :, None], full / jnp.sqrt(jnp.float32(2.0)), full)
    count = (my_end - last_start).astype(jnp.float32)
    cache_state = (full[..., :DV] / count)[None]
    cache_norm = (full[..., DV] / count)[None]

    attn = (numerator_term / denom[:, :, None]).astype(jnp.bfloat16).reshape(nrows, heads * DV)
    mixed_terms = jnp.dot(attn, w_out, preferred_element_type=jnp.float32).astype(jnp.bfloat16)
    mixed_rows = reduce_rows(mixed_terms).astype(jnp.bfloat16)
    mixed = gather_stack(mixed_rows).reshape(nrows, -1).astype(jnp.float32)
    res1 = resid + mixed
    n2 = norm_rows(res1, norm_conv).astype(jnp.bfloat16)
    width = w_proj.shape[1]
    own = lax.dynamic_slice_in_dim(n2, lax.axis_index(MP) * width, width, 1)
    proj = jnp.dot(n2, w_proj, preferred_element_type=jnp.float32)
    rim = shifted(own[nrows - (KC - 1) :], SEQ, 1)
    extended = jnp.concatenate([rim, own], axis=0).astype(jnp.float32)
    conv = jnp.zeros((nrows, width), jnp.float32)
    for tap in range(KC):
        keep = (place - tap >= doc_start).astype(jnp.float32)
        conv = (
            conv
            + conv_kernel[tap].astype(jnp.float32)[None, :]
            * extended[KC - 1 - tap : KC - 1 - tap + nrows]
            * keep[:, None]
        )
    gated = (proj * conv).astype(jnp.bfloat16)
    gathered = gather_stack(gated).transpose(1, 0, 2).reshape(nrows, -1)
    res2 = res1 + gathered.astype(jnp.float32)
    n3 = norm_rows(res2, norm_mlp).astype(jnp.bfloat16)
    gate = jnp.dot(n3, w_gate, preferred_element_type=jnp.float32)
    upper = jnp.dot(n3, w_up, preferred_element_type=jnp.float32)
    hid = (jax.nn.silu(gate) * upper).astype(jnp.bfloat16)
    down_terms = jnp.dot(hid, w_down, preferred_element_type=jnp.float32).astype(jnp.bfloat16)
    res2_rows = (own_rows(resid) + own_rows(mixed)) + own_rows(gathered).astype(jnp.float32)
    out_rows = (res2_rows + reduce_rows(down_terms)).astype(jnp.bfloat16)
    hidden_out = gather_stack(out_rows).reshape(nrows, -1)
    return (hidden_out, cache_state, cache_norm)


def solution(mesh):
    nseq, nmp = mesh.devices.shape
    nx = 4 if nseq % 4 == 0 else 1
    split = jax.sharding.Mesh(
        mesh.devices.reshape(nx, nseq // nx, nmp // 2, 2), ("x", "z", "y", "core")
    )
    return jax.shard_map(
        on_device,
        mesh=split,
        in_specs=(
            P(SEQ, None),
            P(),
            P(),
            P(),
            P(),
            P(None, MP),
            P(None, MP),
            P(None, MP),
            P(MP, None),
            P(None, MP),
            P(None, MP),
            P(None, MP),
            P(None, MP),
            P(MP, None),
        ),
        out_specs=(P(SEQ, None), P(SEQ, MP, None, None), P(SEQ, MP, None)),
        check_vma=False,
    )
```

```python
import jax
import jax.numpy as jnp
import numpy as np
from jax import lax
from jax.sharding import PartitionSpec as P

F = 16
DV = 112
KC = 3
FEAT = 273
MP = ("y", "core")
SEQ = ("x", "z")

PAIR_A, PAIR_B = np.triu_indices(F)
NPAIR = PAIR_A.shape[0]
NCOMP = 1 + F + NPAIR
PAIR_W = np.where(PAIR_A == PAIR_B, 0.5, 1.0).astype(np.float32)


def _feature_maps():
    left = np.zeros((F, NCOMP), np.float32)
    right = np.zeros((F, NCOMP), np.float32)
    left_bias = np.zeros((NCOMP,), np.float32)
    right_bias = np.zeros((NCOMP,), np.float32)
    left_bias[0] = right_bias[0] = 1.0
    for a in range(F):
        left[a, 1 + a] = 1.0
        right_bias[1 + a] = 1.0
    left[PAIR_A, 1 + F + np.arange(NPAIR)] = 1.0
    right[PAIR_B, 1 + F + np.arange(NPAIR)] = 1.0
    right_q = right.copy()
    right_q[PAIR_B, 1 + F + np.arange(NPAIR)] = PAIR_W
    pos = np.zeros((F, F), np.int32)
    pos[PAIR_A, PAIR_B] = np.arange(NPAIR)
    pos[PAIR_B, PAIR_A] = np.arange(NPAIR)
    rows = np.concatenate([np.arange(1 + F), 1 + F + pos.reshape(-1)])
    select = np.zeros((FEAT, NCOMP), np.float32)
    select[np.arange(FEAT), rows] = 1.0
    outer = np.concatenate([np.zeros(1 + F, bool), np.ones(F * F, bool)])
    return left, right, right_q, left_bias, right_bias, select, outer


LEFT, RIGHT, RIGHT_Q, LEFT_BIAS, RIGHT_BIAS, SELECT, EXPAND_OUTER = _feature_maps()


def shifted(value, axis, steps):
    count = lax.axis_size(axis)
    leading, last = (max(0, -steps), min(count, count - steps))
    return lax.ppermute(value, axis, [(source, source + steps) for source in range(leading, last)])


def norm_rows(values, gain):
    mean_sq = jnp.mean(values * values, axis=-1, keepdims=True)
    return values * lax.rsqrt(mean_sq + 1e-06) * gain.astype(jnp.float32)


def compact_features(heads_in, weighted):
    scaled = heads_in * jnp.bfloat16(0.5)
    right = RIGHT_Q if weighted else RIGHT
    lhs = jnp.einsum("nhf,fe->nhe", scaled, jnp.asarray(LEFT, jnp.bfloat16), preferred_element_type=jnp.float32)
    rhs = jnp.einsum("nhf,fe->nhe", scaled, jnp.asarray(right, jnp.bfloat16), preferred_element_type=jnp.float32)
    return (lhs + LEFT_BIAS) * (rhs + RIGHT_BIAS)


def reduce_rows(x):
    core = lax.axis_index("core")
    ny = lax.axis_size("y")
    chunks = x.reshape((ny, 2, -1) + x.shape[1:])
    mine = lax.dynamic_index_in_dim(chunks, core, 1, keepdims=False)
    theirs = lax.dynamic_index_in_dim(chunks, 1 - core, 1, keepdims=False)
    got = lax.ppermute(theirs, "core", [(0, 1), (1, 0)])
    pair = (mine.astype(jnp.float32) + got.astype(jnp.float32)).astype(jnp.bfloat16)
    parts = lax.all_to_all(pair, "y", 0, 0, tiled=False)
    return jnp.sum(parts.astype(jnp.float32), axis=0)


def gather_stack(c):
    core = lax.axis_index("core")
    ny = lax.axis_size("y")
    same = lax.all_to_all(jnp.broadcast_to(c[None], (ny,) + c.shape), "y", 0, 0, tiled=False)
    other = lax.ppermute(same, "core", [(0, 1), (1, 0)])
    out = jnp.zeros((ny, 2) + c.shape, c.dtype)
    out = lax.dynamic_update_index_in_dim(out, same[:, None], core, 1)
    out = lax.dynamic_update_index_in_dim(out, other[:, None], 1 - core, 1)
    return out.reshape((2 * ny,) + c.shape)


def own_rows(x):
    n = lax.axis_size(MP)
    rows = x.shape[0] // n
    return lax.dynamic_slice_in_dim(x, lax.axis_index(MP) * rows, rows, 0)


def pair_weights(query, keys):
    score = jnp.einsum("nhf,mhf->hnm", query, keys, preferred_element_type=jnp.float32) * F ** (
        -0.5
    )
    return 1.0 + score + 0.5 * score * score


def on_device(
    tokens,
    prompt_lengths,
    norm_mixer,
    norm_conv,
    norm_mlp,
    w_query,
    w_key,
    w_value,
    w_out,
    w_proj,
    conv_kernel,
    w_gate,
    w_up,
    w_down,
):
    hp = lax.Precision.HIGHEST
    nrows = tokens.shape[0]
    heads = w_query.shape[1] // F
    nseq = lax.axis_size(SEQ)
    me = lax.axis_index(SEQ)
    my_start = me * nrows
    my_end = my_start + nrows
    place = my_start + jnp.arange(nrows, dtype=jnp.int32)
    ends = jnp.cumsum(prompt_lengths)
    below = ends[None, :] <= place[:, None]
    doc_start = jnp.max(jnp.where(below, ends[None, :], 0), axis=1)
    last_start = doc_start[-1]

    block_first = jnp.arange(nseq, dtype=jnp.int32) * nrows
    block_last_start = jnp.max(
        jnp.where(ends[None, :] <= block_first[:, None] + nrows - 1, ends[None, :], 0), axis=1
    )
    flags = block_last_start < block_first

    resid = tokens.astype(jnp.float32)
    n1 = norm_rows(resid, norm_mixer).astype(jnp.bfloat16)
    query = (
        jnp.dot(n1, w_query, preferred_element_type=jnp.float32)
        .astype(jnp.bfloat16)
        .reshape(nrows, heads, F)
    )
    keys = (
        jnp.dot(n1, w_key, preferred_element_type=jnp.float32)
        .astype(jnp.bfloat16)
        .reshape(nrows, heads, F)
    )
    values = (
        jnp.dot(n1, w_value, preferred_element_type=jnp.float32)
        .astype(jnp.bfloat16)
        .reshape(nrows, heads, DV)
    )
    values_f = values.astype(jnp.float32)

    tail = (place >= last_start).astype(jnp.float32)
    phik = compact_features(keys, False) * tail[:, None, None]
    v_aug = jnp.concatenate([values_f, jnp.ones((nrows, heads, 1), jnp.float32)], axis=-1)
    local_state = jnp.einsum("nhe,nhd->hed", phik, v_aug, precision=hp)

    breaks = jnp.cumsum((~flags).astype(jnp.int32))

    def breaks_at(i):
        return jnp.where(i >= 0, breaks[jnp.maximum(i, 0)], 0)

    def chain(upto, first_block, count, stride, stack):
        index = jnp.arange(count, dtype=jnp.int32)
        last_of = first_block + index * stride + stride - 1
        keep = (last_of <= upto) & (breaks_at(upto) == breaks_at(last_of))
        return jnp.einsum(
            "s,shed->hed", keep.astype(jnp.bfloat16), stack, preferred_element_type=jnp.float32
        )

    nz = lax.axis_size("z")
    nx = lax.axis_size("x")
    group = lax.axis_index("x")
    group_first = group * nz
    payload = local_state.astype(jnp.bfloat16)
    members = lax.all_to_all(jnp.broadcast_to(payload[None], (nz,) + payload.shape), "z", 0, 0, tiled=False)
    within = chain(me - 1, group_first, nz, 1, members)
    group_end = chain(group_first + nz - 1, group_first, nz, 1, members).astype(jnp.bfloat16)
    ends_all = lax.all_to_all(jnp.broadcast_to(group_end[None], (nx,) + group_end.shape), "x", 0, 0, tiled=False)
    carry_in = chain(group_first - 1, 0, nx, nz, ends_all)
    into_block = (breaks_at(me - 1) == breaks_at(group_first - 1)).astype(jnp.float32)
    carried = within + into_block * carry_in

    local_mask = (place[None, :] <= place[:, None]) & (place[None, :] >= doc_start[:, None])
    weight_matrix = pair_weights(query, keys) * local_mask.astype(jnp.float32)[None]
    numerator_term = jnp.einsum("hnm,mhd->nhd", weight_matrix, values_f, precision=hp)
    denom = jnp.sum(weight_matrix, axis=2).T

    apply = (doc_start < my_start).astype(jnp.float32)
    phiq = compact_features(query, True)
    cross = (
        jnp.einsum("nhe,hed->nhd", phiq, within, precision=hp)
        + into_block * jnp.einsum("nhe,hed->nhd", phiq, carry_in, precision=hp)
    ) * apply[:, None, None]
    numerator_term = numerator_term + cross[..., :DV]
    denom = denom + cross[..., DV]

    own_flag = flags[me].astype(jnp.float32)
    total = local_state + own_flag * carried
    full = jnp.einsum("re,hed->hrd", SELECT, total, precision=hp)
    full = jnp.where(EXPAND_OUTER[None, :, None], full / jnp.sqrt(jnp.float32(2.0)), full)
    count = (my_end - last_start).astype(jnp.float32)
    cache_state = (full[..., :DV] / count)[None]
    cache_norm = (full[..., DV] / count)[None]

    attn = (numerator_term / denom[:, :, None]).astype(jnp.bfloat16).reshape(nrows, heads * DV)
    mixed_terms = jnp.dot(attn, w_out, preferred_element_type=jnp.float32).astype(jnp.bfloat16)
    mixed_rows = reduce_rows(mixed_terms).astype(jnp.bfloat16)
    mixed = gather_stack(mixed_rows).reshape(nrows, -1).astype(jnp.float32)
    res1 = resid + mixed
    n2 = norm_rows(res1, norm_conv).astype(jnp.bfloat16)
    width = w_proj.shape[1]
    own = lax.dynamic_slice_in_dim(n2, lax.axis_index(MP) * width, width, 1)
    proj = jnp.dot(n2, w_proj, preferred_element_type=jnp.float32)
    rim = shifted(own[nrows - (KC - 1) :], SEQ, 1)
    extended = jnp.concatenate([rim, own], axis=0).astype(jnp.float32)
    conv = jnp.zeros((nrows, width), jnp.float32)
    for tap in range(KC):
        keep = (place - tap >= doc_start).astype(jnp.float32)
        conv = (
            conv
            + conv_kernel[tap].astype(jnp.float32)[None, :]
            * extended[KC - 1 - tap : KC - 1 - tap + nrows]
            * keep[:, None]
        )
    gated = (proj * conv).astype(jnp.bfloat16)
    gathered = gather_stack(gated).transpose(1, 0, 2).reshape(nrows, -1)
    res2 = res1 + gathered.astype(jnp.float32)
    n3 = norm_rows(res2, norm_mlp).astype(jnp.bfloat16)
    gate = jnp.dot(n3, w_gate, preferred_element_type=jnp.float32)
    upper = jnp.dot(n3, w_up, preferred_element_type=jnp.float32)
    hid = (jax.nn.silu(gate) * upper).astype(jnp.bfloat16)
    down_terms = jnp.dot(hid, w_down, preferred_element_type=jnp.float32).astype(jnp.bfloat16)
    out_rows = (own_rows(res2) + reduce_rows(down_terms)).astype(jnp.bfloat16)
    hidden_out = gather_stack(out_rows).reshape(nrows, -1)
    return (hidden_out, cache_state, cache_norm)


def solution(mesh):
    nseq, nmp = mesh.devices.shape
    nx = 4 if nseq % 4 == 0 else 1
    split = jax.sharding.Mesh(
        mesh.devices.reshape(nx, nseq // nx, nmp // 2, 2), ("x", "z", "y", "core")
    )
    return jax.shard_map(
        on_device,
        mesh=split,
        in_specs=(
            P(SEQ, None),
            P(),
            P(),
            P(),
            P(),
            P(None, MP),
            P(None, MP),
            P(None, MP),
            P(MP, None),
            P(None, MP),
            P(None, MP),
            P(None, MP),
            P(None, MP),
            P(MP, None),
        ),
        out_specs=(P(SEQ, None), P(SEQ, MP, None, None), P(SEQ, MP, None)),
        check_vma=False,
    )
```

```python
import jax
import jax.numpy as jnp
import numpy as np
from jax import lax
from jax.sharding import PartitionSpec as P

F = 16
DV = 112
KC = 3
FEAT = 273
MP = ("y", "core")
SEQ = ("x", "z")

PAIR_A, PAIR_B = np.triu_indices(F)
NPAIR = PAIR_A.shape[0]
NCOMP = 1 + F + NPAIR
PAIR_W = np.where(PAIR_A == PAIR_B, 0.5, 1.0).astype(np.float32)


def _feature_maps():
    left = np.zeros((F, NCOMP), np.float32)
    right = np.zeros((F, NCOMP), np.float32)
    left_bias = np.zeros((NCOMP,), np.float32)
    right_bias = np.zeros((NCOMP,), np.float32)
    left_bias[0] = right_bias[0] = 1.0
    for a in range(F):
        left[a, 1 + a] = 1.0
        right_bias[1 + a] = 1.0
    left[PAIR_A, 1 + F + np.arange(NPAIR)] = 1.0
    right[PAIR_B, 1 + F + np.arange(NPAIR)] = 1.0
    right_q = right.copy()
    right_q[PAIR_B, 1 + F + np.arange(NPAIR)] = PAIR_W
    pos = np.zeros((F, F), np.int32)
    pos[PAIR_A, PAIR_B] = np.arange(NPAIR)
    pos[PAIR_B, PAIR_A] = np.arange(NPAIR)
    rows = np.concatenate([np.arange(1 + F), 1 + F + pos.reshape(-1)])
    select = np.zeros((FEAT, NCOMP), np.float32)
    select[np.arange(FEAT), rows] = 1.0
    outer = np.concatenate([np.zeros(1 + F, bool), np.ones(F * F, bool)])
    return left, right, right_q, left_bias, right_bias, select, outer


LEFT, RIGHT, RIGHT_Q, LEFT_BIAS, RIGHT_BIAS, SELECT, EXPAND_OUTER = _feature_maps()


def shifted(value, axis, steps):
    count = lax.axis_size(axis)
    leading, last = (max(0, -steps), min(count, count - steps))
    return lax.ppermute(value, axis, [(source, source + steps) for source in range(leading, last)])


def norm_rows(values, gain):
    mean_sq = jnp.mean(values * values, axis=-1, keepdims=True)
    return values * lax.rsqrt(mean_sq + 1e-06) * gain.astype(jnp.float32)


def compact_features(heads_in, weighted):
    scaled = heads_in * jnp.bfloat16(0.5)
    right = RIGHT_Q if weighted else RIGHT
    lhs = jnp.einsum("nhf,fe->nhe", scaled, jnp.asarray(LEFT, jnp.bfloat16), preferred_element_type=jnp.float32)
    rhs = jnp.einsum("nhf,fe->nhe", scaled, jnp.asarray(right, jnp.bfloat16), preferred_element_type=jnp.float32)
    return (lhs + LEFT_BIAS) * (rhs + RIGHT_BIAS)


def reduce_rows(x):
    core = lax.axis_index("core")
    ny = lax.axis_size("y")
    chunks = x.reshape((ny, 2, -1) + x.shape[1:])
    mine = lax.dynamic_index_in_dim(chunks, core, 1, keepdims=False)
    theirs = lax.dynamic_index_in_dim(chunks, 1 - core, 1, keepdims=False)
    got = lax.ppermute(theirs, "core", [(0, 1), (1, 0)])
    pair = (mine.astype(jnp.float32) + got.astype(jnp.float32)).astype(jnp.bfloat16)
    parts = lax.all_to_all(pair, "y", 0, 0, tiled=False)
    return jnp.sum(parts.astype(jnp.float32), axis=0)


def gather_stack(c):
    core = lax.axis_index("core")
    ny = lax.axis_size("y")
    same = lax.all_to_all(jnp.broadcast_to(c[None], (ny,) + c.shape), "y", 0, 0, tiled=False)
    other = lax.ppermute(same, "core", [(0, 1), (1, 0)])
    out = jnp.zeros((ny, 2) + c.shape, c.dtype)
    out = lax.dynamic_update_index_in_dim(out, same[:, None], core, 1)
    out = lax.dynamic_update_index_in_dim(out, other[:, None], 1 - core, 1)
    return out.reshape((2 * ny,) + c.shape)


def own_rows(x):
    n = lax.axis_size(MP)
    rows = x.shape[0] // n
    return lax.dynamic_slice_in_dim(x, lax.axis_index(MP) * rows, rows, 0)


def pair_weights(query, keys):
    score = jnp.einsum("nhf,mhf->hnm", query, keys, preferred_element_type=jnp.float32) * F ** (
        -0.5
    )
    return 1.0 + score + 0.5 * score * score


def on_device(
    tokens,
    prompt_lengths,
    norm_mixer,
    norm_conv,
    norm_mlp,
    w_query,
    w_key,
    w_value,
    w_out,
    w_proj,
    conv_kernel,
    w_gate,
    w_up,
    w_down,
):
    hp = lax.Precision.HIGHEST
    nrows = tokens.shape[0]
    heads = w_query.shape[1] // F
    nseq = lax.axis_size(SEQ)
    me = lax.axis_index(SEQ)
    my_start = me * nrows
    my_end = my_start + nrows
    place = my_start + jnp.arange(nrows, dtype=jnp.int32)
    ends = jnp.cumsum(prompt_lengths)
    below = ends[None, :] <= place[:, None]
    doc_start = jnp.max(jnp.where(below, ends[None, :], 0), axis=1)
    last_start = doc_start[-1]

    block_first = jnp.arange(nseq, dtype=jnp.int32) * nrows
    block_last_start = jnp.max(
        jnp.where(ends[None, :] <= block_first[:, None] + nrows - 1, ends[None, :], 0), axis=1
    )
    flags = block_last_start < block_first

    resid = tokens.astype(jnp.float32)
    n1 = norm_rows(resid, norm_mixer).astype(jnp.bfloat16)
    query = (
        jnp.dot(n1, w_query, preferred_element_type=jnp.float32)
        .astype(jnp.bfloat16)
        .reshape(nrows, heads, F)
    )
    keys = (
        jnp.dot(n1, w_key, preferred_element_type=jnp.float32)
        .astype(jnp.bfloat16)
        .reshape(nrows, heads, F)
    )
    values = (
        jnp.dot(n1, w_value, preferred_element_type=jnp.float32)
        .astype(jnp.bfloat16)
        .reshape(nrows, heads, DV)
    )
    values_f = values.astype(jnp.float32)

    tail = (place >= last_start).astype(jnp.float32)
    phik = compact_features(keys, False) * tail[:, None, None]
    v_aug = jnp.concatenate([values_f, jnp.ones((nrows, heads, 1), jnp.float32)], axis=-1)
    local_state = jnp.einsum("nhe,nhd->hed", phik, v_aug, precision=hp)

    breaks = jnp.cumsum((~flags).astype(jnp.int32))

    def breaks_at(i):
        return jnp.where(i >= 0, breaks[jnp.maximum(i, 0)], 0)

    def chain(upto, first_block, count, stride, stack):
        index = jnp.arange(count, dtype=jnp.int32)
        last_of = first_block + index * stride + stride - 1
        keep = (last_of <= upto) & (breaks_at(upto) == breaks_at(last_of))
        return jnp.einsum(
            "s,sab->ab", keep.astype(jnp.bfloat16), stack, preferred_element_type=jnp.float32
        )

    nz = lax.axis_size("z")
    nx = lax.axis_size("x")
    group = lax.axis_index("x")
    group_first = group * nz
    state_size = local_state.size
    lanes = 128
    flat_rows = -(-state_size // lanes)
    payload = jnp.pad(
        local_state.astype(jnp.bfloat16).reshape(-1), (0, flat_rows * lanes - state_size)
    ).reshape(flat_rows, lanes)
    members = lax.all_to_all(jnp.broadcast_to(payload[None], (nz,) + payload.shape), "z", 0, 0, tiled=False)
    within = chain(me - 1, group_first, nz, 1, members)
    group_end = chain(group_first + nz - 1, group_first, nz, 1, members).astype(jnp.bfloat16)
    ends_all = lax.all_to_all(jnp.broadcast_to(group_end[None], (nx,) + group_end.shape), "x", 0, 0, tiled=False)
    carry_in = chain(group_first - 1, 0, nx, nz, ends_all)
    into_block = (breaks_at(me - 1) == breaks_at(group_first - 1)).astype(jnp.float32)
    carried = (within + into_block * carry_in).reshape(-1)[:state_size].reshape(local_state.shape)

    local_mask = (place[None, :] <= place[:, None]) & (place[None, :] >= doc_start[:, None])
    weight_matrix = pair_weights(query, keys) * local_mask.astype(jnp.float32)[None]
    numerator_term = jnp.einsum("hnm,mhd->nhd", weight_matrix, values_f, precision=hp)
    denom = jnp.sum(weight_matrix, axis=2).T

    apply = (doc_start < my_start).astype(jnp.float32)
    phiq = compact_features(query, True)
    cross = jnp.einsum("nhe,hed->nhd", phiq, carried, precision=hp) * apply[:, None, None]
    numerator_term = numerator_term + cross[..., :DV]
    denom = denom + cross[..., DV]

    own_flag = flags[me].astype(jnp.float32)
    total = local_state + own_flag * carried
    full = jnp.einsum("re,hed->hrd", SELECT, total, precision=hp)
    full = jnp.where(EXPAND_OUTER[None, :, None], full / jnp.sqrt(jnp.float32(2.0)), full)
    count = (my_end - last_start).astype(jnp.float32)
    cache_state = (full[..., :DV] / count)[None]
    cache_norm = (full[..., DV] / count)[None]

    attn = (numerator_term / denom[:, :, None]).astype(jnp.bfloat16).reshape(nrows, heads * DV)
    mixed_terms = jnp.dot(attn, w_out, preferred_element_type=jnp.float32).astype(jnp.bfloat16)
    mixed_rows = reduce_rows(mixed_terms).astype(jnp.bfloat16)
    mixed = gather_stack(mixed_rows).reshape(nrows, -1).astype(jnp.float32)
    res1 = resid + mixed
    n2 = norm_rows(res1, norm_conv).astype(jnp.bfloat16)
    width = w_proj.shape[1]
    own = lax.dynamic_slice_in_dim(n2, lax.axis_index(MP) * width, width, 1)
    proj = jnp.dot(n2, w_proj, preferred_element_type=jnp.float32)
    rim = shifted(own[nrows - (KC - 1) :], SEQ, 1)
    extended = jnp.concatenate([rim, own], axis=0).astype(jnp.float32)
    conv = jnp.zeros((nrows, width), jnp.float32)
    for tap in range(KC):
        keep = (place - tap >= doc_start).astype(jnp.float32)
        conv = (
            conv
            + conv_kernel[tap].astype(jnp.float32)[None, :]
            * extended[KC - 1 - tap : KC - 1 - tap + nrows]
            * keep[:, None]
        )
    gated = (proj * conv).astype(jnp.bfloat16)
    gathered = gather_stack(gated).transpose(1, 0, 2).reshape(nrows, -1)
    res2 = res1 + gathered.astype(jnp.float32)
    n3 = norm_rows(res2, norm_mlp).astype(jnp.bfloat16)
    gate = jnp.dot(n3, w_gate, preferred_element_type=jnp.float32)
    upper = jnp.dot(n3, w_up, preferred_element_type=jnp.float32)
    hid = (jax.nn.silu(gate) * upper).astype(jnp.bfloat16)
    down_terms = jnp.dot(hid, w_down, preferred_element_type=jnp.float32).astype(jnp.bfloat16)
    out_rows = (own_rows(res2) + reduce_rows(down_terms)).astype(jnp.bfloat16)
    hidden_out = gather_stack(out_rows).reshape(nrows, -1)
    return (hidden_out, cache_state, cache_norm)


def solution(mesh):
    nseq, nmp = mesh.devices.shape
    nx = 4 if nseq % 4 == 0 else 1
    split = jax.sharding.Mesh(
        mesh.devices.reshape(nx, nseq // nx, nmp // 2, 2), ("x", "z", "y", "core")
    )
    return jax.shard_map(
        on_device,
        mesh=split,
        in_specs=(
            P(SEQ, None),
            P(),
            P(),
            P(),
            P(),
            P(None, MP),
            P(None, MP),
            P(None, MP),
            P(MP, None),
            P(None, MP),
            P(None, MP),
            P(None, MP),
            P(None, MP),
            P(MP, None),
        ),
        out_specs=(P(SEQ, None), P(SEQ, MP, None, None), P(SEQ, MP, None)),
        check_vma=False,
    )
```

```python
import jax
import jax.numpy as jnp
import numpy as np
from jax import lax
from jax.sharding import PartitionSpec as P

F = 16
DV = 112
KC = 3
FEAT = 273
MP = ("y", "core")
SEQ = ("x", "z")

PAIR_A, PAIR_B = np.triu_indices(F)
NPAIR = PAIR_A.shape[0]
NCOMP = 1 + F + NPAIR
PAIR_W = np.where(PAIR_A == PAIR_B, 0.5, 1.0).astype(np.float32)


def _feature_maps():
    left = np.zeros((F, NCOMP), np.float32)
    right = np.zeros((F, NCOMP), np.float32)
    left_bias = np.zeros((NCOMP,), np.float32)
    right_bias = np.zeros((NCOMP,), np.float32)
    left_bias[0] = right_bias[0] = 1.0
    for a in range(F):
        left[a, 1 + a] = 1.0
        right_bias[1 + a] = 1.0
    left[PAIR_A, 1 + F + np.arange(NPAIR)] = 1.0
    right[PAIR_B, 1 + F + np.arange(NPAIR)] = 1.0
    right_q = right.copy()
    right_q[PAIR_B, 1 + F + np.arange(NPAIR)] = PAIR_W
    pos = np.zeros((F, F), np.int32)
    pos[PAIR_A, PAIR_B] = np.arange(NPAIR)
    pos[PAIR_B, PAIR_A] = np.arange(NPAIR)
    rows = np.concatenate([np.arange(1 + F), 1 + F + pos.reshape(-1)])
    select = np.zeros((FEAT, NCOMP), np.float32)
    select[np.arange(FEAT), rows] = 1.0
    outer = np.concatenate([np.zeros(1 + F, bool), np.ones(F * F, bool)])
    return left, right, right_q, left_bias, right_bias, select, outer


LEFT, RIGHT, RIGHT_Q, LEFT_BIAS, RIGHT_BIAS, SELECT, EXPAND_OUTER = _feature_maps()


def shifted(value, axis, steps):
    count = lax.axis_size(axis)
    leading, last = (max(0, -steps), min(count, count - steps))
    return lax.ppermute(value, axis, [(source, source + steps) for source in range(leading, last)])


def norm_rows(values, gain):
    mean_sq = jnp.mean(values * values, axis=-1, keepdims=True)
    return values * lax.rsqrt(mean_sq + 1e-06) * gain.astype(jnp.float32)


def compact_features(heads_in, weighted):
    scaled = heads_in * jnp.bfloat16(0.5)
    right = RIGHT_Q if weighted else RIGHT
    lhs = jnp.einsum("nhf,fe->nhe", scaled, jnp.asarray(LEFT, jnp.bfloat16), preferred_element_type=jnp.float32)
    rhs = jnp.einsum("nhf,fe->nhe", scaled, jnp.asarray(right, jnp.bfloat16), preferred_element_type=jnp.float32)
    return (lhs + LEFT_BIAS) * (rhs + RIGHT_BIAS)


def reduce_rows(x):
    core = lax.axis_index("core")
    ny = lax.axis_size("y")
    chunks = x.reshape((ny, 2, -1) + x.shape[1:])
    mine = lax.dynamic_index_in_dim(chunks, core, 1, keepdims=False)
    theirs = lax.dynamic_index_in_dim(chunks, 1 - core, 1, keepdims=False)
    got = lax.ppermute(theirs, "core", [(0, 1), (1, 0)])
    pair = (mine.astype(jnp.float32) + got.astype(jnp.float32)).astype(jnp.bfloat16)
    parts = lax.all_to_all(pair, "y", 0, 0, tiled=False)
    return jnp.sum(parts.astype(jnp.float32), axis=0)


def gather_stack(c):
    core = lax.axis_index("core")
    ny = lax.axis_size("y")
    same = lax.all_to_all(jnp.broadcast_to(c[None], (ny,) + c.shape), "y", 0, 0, tiled=False)
    other = lax.ppermute(same, "core", [(0, 1), (1, 0)])
    out = jnp.zeros((ny, 2) + c.shape, c.dtype)
    out = lax.dynamic_update_index_in_dim(out, same[:, None], core, 1)
    out = lax.dynamic_update_index_in_dim(out, other[:, None], 1 - core, 1)
    return out.reshape((2 * ny,) + c.shape)


def own_rows(x):
    n = lax.axis_size(MP)
    rows = x.shape[0] // n
    return lax.dynamic_slice_in_dim(x, lax.axis_index(MP) * rows, rows, 0)


def pair_weights(query, keys):
    score = jnp.einsum("nhf,mhf->hnm", query, keys, preferred_element_type=jnp.float32) * F ** (
        -0.5
    )
    return 1.0 + score + 0.5 * score * score


def on_device(
    tokens,
    prompt_lengths,
    norm_mixer,
    norm_conv,
    norm_mlp,
    w_query,
    w_key,
    w_value,
    w_out,
    w_proj,
    conv_kernel,
    w_gate,
    w_up,
    w_down,
):
    hp = lax.Precision.HIGHEST
    nrows = tokens.shape[0]
    heads = w_query.shape[1] // F
    nseq = lax.axis_size(SEQ)
    me = lax.axis_index(SEQ)
    my_start = me * nrows
    my_end = my_start + nrows
    place = my_start + jnp.arange(nrows, dtype=jnp.int32)
    ends = jnp.cumsum(prompt_lengths)
    below = ends[None, :] <= place[:, None]
    doc_start = jnp.max(jnp.where(below, ends[None, :], 0), axis=1)
    last_start = doc_start[-1]

    block_first = jnp.arange(nseq, dtype=jnp.int32) * nrows
    block_last_start = jnp.max(
        jnp.where(ends[None, :] <= block_first[:, None] + nrows - 1, ends[None, :], 0), axis=1
    )
    flags = block_last_start < block_first

    resid = tokens.astype(jnp.float32)
    n1 = norm_rows(resid, norm_mixer).astype(jnp.bfloat16)
    query = (
        jnp.dot(n1, w_query, preferred_element_type=jnp.float32)
        .astype(jnp.bfloat16)
        .reshape(nrows, heads, F)
    )
    keys = (
        jnp.dot(n1, w_key, preferred_element_type=jnp.float32)
        .astype(jnp.bfloat16)
        .reshape(nrows, heads, F)
    )
    values = (
        jnp.dot(n1, w_value, preferred_element_type=jnp.float32)
        .astype(jnp.bfloat16)
        .reshape(nrows, heads, DV)
    )
    values_f = values.astype(jnp.float32)

    tail = (place >= last_start).astype(jnp.float32)
    phik = compact_features(keys, False) * tail[:, None, None]
    v_aug = jnp.concatenate([values_f, jnp.ones((nrows, heads, 1), jnp.float32)], axis=-1)
    phik_hi = phik.astype(jnp.bfloat16)
    phik_lo = (phik - phik_hi.astype(jnp.float32)).astype(jnp.bfloat16)
    v_aug_b = v_aug.astype(jnp.bfloat16)
    local_state = jnp.einsum(
        "nhe,nhd->hed", phik_hi, v_aug_b, preferred_element_type=jnp.float32
    ) + jnp.einsum("nhe,nhd->hed", phik_lo, v_aug_b, preferred_element_type=jnp.float32)

    breaks = jnp.cumsum((~flags).astype(jnp.int32))

    def breaks_at(i):
        return jnp.where(i >= 0, breaks[jnp.maximum(i, 0)], 0)

    def chain(upto, first_block, count, stride, stack):
        index = jnp.arange(count, dtype=jnp.int32)
        last_of = first_block + index * stride + stride - 1
        keep = (last_of <= upto) & (breaks_at(upto) == breaks_at(last_of))
        return jnp.einsum(
            "s,sab->ab", keep.astype(jnp.bfloat16), stack, preferred_element_type=jnp.float32
        )

    nz = lax.axis_size("z")
    nx = lax.axis_size("x")
    group = lax.axis_index("x")
    group_first = group * nz
    state_size = local_state.size
    lanes = 128
    flat_rows = -(-state_size // lanes)
    payload = jnp.pad(
        local_state.astype(jnp.bfloat16).reshape(-1), (0, flat_rows * lanes - state_size)
    ).reshape(flat_rows, lanes)
    members = lax.all_to_all(jnp.broadcast_to(payload[None], (nz,) + payload.shape), "z", 0, 0, tiled=False)
    within = chain(me - 1, group_first, nz, 1, members)
    group_end = chain(group_first + nz - 1, group_first, nz, 1, members).astype(jnp.bfloat16)
    ends_all = lax.all_to_all(jnp.broadcast_to(group_end[None], (nx,) + group_end.shape), "x", 0, 0, tiled=False)
    carry_in = chain(group_first - 1, 0, nx, nz, ends_all)
    into_block = (breaks_at(me - 1) == breaks_at(group_first - 1)).astype(jnp.float32)
    carried = (within + into_block * carry_in).reshape(-1)[:state_size].reshape(local_state.shape)

    local_mask = (place[None, :] <= place[:, None]) & (place[None, :] >= doc_start[:, None])
    weight_matrix = pair_weights(query, keys) * local_mask.astype(jnp.float32)[None]
    numerator_term = jnp.einsum("hnm,mhd->nhd", weight_matrix, values_f, precision=hp)
    denom = jnp.sum(weight_matrix, axis=2).T

    apply = (doc_start < my_start).astype(jnp.float32)
    phiq = compact_features(query, True)
    cross = jnp.einsum("nhe,hed->nhd", phiq, carried, precision=hp) * apply[:, None, None]
    numerator_term = numerator_term + cross[..., :DV]
    denom = denom + cross[..., DV]

    own_flag = flags[me].astype(jnp.float32)
    total = local_state + own_flag * carried
    full = jnp.einsum("re,hed->hrd", SELECT, total, precision=hp)
    full = jnp.where(EXPAND_OUTER[None, :, None], full / jnp.sqrt(jnp.float32(2.0)), full)
    count = (my_end - last_start).astype(jnp.float32)
    cache_state = (full[..., :DV] / count)[None]
    cache_norm = (full[..., DV] / count)[None]

    attn = (numerator_term / denom[:, :, None]).astype(jnp.bfloat16).reshape(nrows, heads * DV)
    mixed_terms = jnp.dot(attn, w_out, preferred_element_type=jnp.float32).astype(jnp.bfloat16)
    mixed_rows = reduce_rows(mixed_terms).astype(jnp.bfloat16)
    mixed = gather_stack(mixed_rows).reshape(nrows, -1).astype(jnp.float32)
    res1 = resid + mixed
    n2 = norm_rows(res1, norm_conv).astype(jnp.bfloat16)
    width = w_proj.shape[1]
    own = lax.dynamic_slice_in_dim(n2, lax.axis_index(MP) * width, width, 1)
    proj = jnp.dot(n2, w_proj, preferred_element_type=jnp.float32)
    rim = shifted(own[nrows - (KC - 1) :], SEQ, 1)
    extended = jnp.concatenate([rim, own], axis=0).astype(jnp.float32)
    conv = jnp.zeros((nrows, width), jnp.float32)
    for tap in range(KC):
        keep = (place - tap >= doc_start).astype(jnp.float32)
        conv = (
            conv
            + conv_kernel[tap].astype(jnp.float32)[None, :]
            * extended[KC - 1 - tap : KC - 1 - tap + nrows]
            * keep[:, None]
        )
    gated = (proj * conv).astype(jnp.bfloat16)
    gathered = gather_stack(gated).transpose(1, 0, 2).reshape(nrows, -1)
    res2 = res1 + gathered.astype(jnp.float32)
    n3 = norm_rows(res2, norm_mlp).astype(jnp.bfloat16)
    gate = jnp.dot(n3, w_gate, preferred_element_type=jnp.float32)
    upper = jnp.dot(n3, w_up, preferred_element_type=jnp.float32)
    hid = (jax.nn.silu(gate) * upper).astype(jnp.bfloat16)
    down_terms = jnp.dot(hid, w_down, preferred_element_type=jnp.float32).astype(jnp.bfloat16)
    out_rows = (own_rows(res2) + reduce_rows(down_terms)).astype(jnp.bfloat16)
    hidden_out = gather_stack(out_rows).reshape(nrows, -1)
    return (hidden_out, cache_state, cache_norm)


def solution(mesh):
    nseq, nmp = mesh.devices.shape
    nx = 4 if nseq % 4 == 0 else 1
    split = jax.sharding.Mesh(
        mesh.devices.reshape(nx, nseq // nx, nmp // 2, 2), ("x", "z", "y", "core")
    )
    return jax.shard_map(
        on_device,
        mesh=split,
        in_specs=(
            P(SEQ, None),
            P(),
            P(),
            P(),
            P(),
            P(None, MP),
            P(None, MP),
            P(None, MP),
            P(MP, None),
            P(None, MP),
            P(None, MP),
            P(None, MP),
            P(None, MP),
            P(MP, None),
        ),
        out_specs=(P(SEQ, None), P(SEQ, MP, None, None), P(SEQ, MP, None)),
        check_vma=False,
    )
```
